32 devices in a mesh: blk: 16 (over z, y, x), band: 2 (over core).
Axes of the slice: x: 2, y: 2, z: 4, core: 2. Of those that a mesh axis runs over, the one named last changes fastest.
Arguments:
- traces: bfloat16 [1024, 2, 8192], P('blk', None, 'band'), may hold values from -80 to 80
- sources: bfloat16 [32, 2, 8192], P('blk', None, 'band'), may hold values from -80 to 80
- owner: int32 [1024, 1], P('blk'), may hold values from 0 to 15; in each aligned block of 64 rows (0 to 63, 64 to 127, ...) at most 8 rows name the same one
Outputs:
- gathers: float32 [32, 4, 128, 256], P('blk', None, 'band')
The draws below stay inside these ranges and needn't reach their ends.
Inputs may be any that keep to these rules, and one draw needn't show every extreme that they name: Among the 64 stations of one device's rows, at most 8 name the same owner block, and some owner block is named by exactly 8 of them in every draw.
All inputs are finite; a program needn't handle non-finite values.
Results may differ from the reference program's by a relative error of at most 0.017.
Values may be sent and summed in bfloat16 or wider, within the bound.
No kernel may reach another device: no remote copies, remote signals or barrier semaphores. Data moves between devices by JAX's collectives and lax.ppermute only.
A program may use at most 128 MiB of HBM per device.

```python
import math
import jax
import jax.numpy as jnp
import numpy as np
from jax import lax

BINS = 8192
DEC = 8
ST_DEV = 64
VS = 2
CAP = 8
RSLOTS = 128
STATIONS = 1024
SOURCES = 32
Q = 4
GROUP_BINS = 4096
OUT = 256
N_BLK = 16
N_BAND = 2


def random_spectrum_rows(key, row_total):
    base_key, scale_key = jax.random.split(key)
    position = jnp.arange(BINS, dtype=jnp.float32) / BINS
    values = jnp.clip(jax.random.normal(base_key, (row_total, 2, BINS), jnp.float32), -5.0, 5.0)
    profile = 1.6 - 1.2 * position
    row_scale = jnp.exp(jax.random.uniform(scale_key, (row_total, 1, 1), jnp.float32) * math.log(10.0))
    return (values * profile[None, None, :] * row_scale).astype(jnp.bfloat16)


def draw_traces(key, part):
    return random_spectrum_rows(jax.random.fold_in(key, 11), STATIONS)


def draw_sources(key, part):
    return random_spectrum_rows(jax.random.fold_in(key, 23), SOURCES)


def shared_out(stream_key, own, number, rows, number_of, top, bound, skew):
    sequence = jax.random.permutation(stream_key, number_of)
    heavy_load, ordinary = load_shares(number_of, rows * top, bound, skew, True), load_shares(number_of, rows * top, bound, skew, False)
    places = jnp.arange(number_of)

    def named(sizes, rotation):
        used = int((sizes > 0).sum())
        fixed = max(1, used // 4)
        passed = fixed + (places - fixed + rotation * (used - fixed)) % max(1, number_of - fixed)
        return jnp.zeros((number_of,), jnp.int32).at[sequence[jnp.where(places < fixed, places, passed)]].set(jnp.asarray(sizes, jnp.int32))

    sizes = jnp.where(number % 4 == 0, named(heavy_load, number // 4), named(ordinary, number - number // 4 - 1))
    mixed = jax.random.permutation(jax.random.fold_in(own, 3), number_of)
    donor, taker = mixed[0:number_of // 2 * 2:2], mixed[1:number_of // 2 * 2:2]
    slack = jnp.minimum(sizes[donor] - 1, bound - sizes[taker]) // 2
    slack = jnp.where((donor == sequence[0]) | (taker == sequence[0]) | (sizes[taker] == 0), 0, jnp.maximum(slack, 0))
    passed = jax.random.randint(jax.random.fold_in(own, 4), (number_of // 2,), 0, 1 << 20) % (slack + 1)
    sizes = sizes.at[donor].add(-passed).at[taker].add(passed)
    items = jnp.searchsorted(jnp.cumsum(sizes), jnp.arange(rows * top), side="right").astype(jnp.int32)
    grid = items.reshape(top, rows).T
    grid = grid[jax.random.permutation(jax.random.fold_in(own, 1), rows)]
    rotation = jax.random.randint(jax.random.fold_in(own, 2), (rows, 1), 0, top)
    return jnp.take_along_axis(grid, (jnp.arange(top)[None, :] + rotation) % top, axis=1)


def load_shares(count, total, reach, lean, full):
    loads = [(1 << 20) // math.isqrt(standing ** lean) + 1 for standing in range(1, count + 1)]
    largest = reach if full else min(reach, max(-(-total // count), total * loads[0] // sum(loads)))
    least = 1 if total - largest >= count - 1 else 0
    holding, surplus = [largest] + [least] * (count - 1), total - largest - least * (count - 1)
    while surplus > 0:
        movable = [i for i in range(1, count) if holding[i] < largest] or [i for i in range(1, count) if holding[i] < reach]
        pool, budget = sum([loads[i] for i in movable]), surplus
        for i in movable:
            more = min(reach - holding[i], max(1, budget * loads[i] // pool), surplus)
            holding[i] = holding[i] + more
            surplus = surplus - more
    return np.array(holding)


def setup_inputs(seed: int = 0) -> dict:
    key_list = jax.random.split(jax.random.key(seed), 4)
    traces = draw_traces(jax.random.fold_in(key_list[3], 71), 0)
    sources = draw_sources(jax.random.fold_in(key_list[3], 71), 0)
    owner_keys = jax.random.split(jax.random.fold_in(key_list[2], 1), STATIONS // ST_DEV)
    owner_turns = jax.random.permutation(jax.random.fold_in(key_list[2], 3), STATIONS // ST_DEV)
    owner = jax.vmap(lambda own, number: shared_out(jax.random.fold_in(key_list[2], 2), own, number, ST_DEV, N_BLK, 1, CAP, 2))(owner_keys, owner_turns).reshape((STATIONS, 1))
    return {"traces": traces, "sources": sources, "owner": owner}


EPS = 1e-06

def whiten(spectrum_rows):
    values = spectrum_rows.astype(jnp.float32)
    power = lax.optimization_barrier(jnp.mean(values * values, axis=(1, 2)))
    return (values * lax.rsqrt(power + EPS)[:, None, None]).astype(jnp.bfloat16)

def reference(traces, sources, owner):
    white_traces = whiten(traces)
    white_sources = whiten(sources)
    owner_flat = owner[:, 0].astype(jnp.int32)
    owner_blocks = owner_flat.reshape(N_BLK, ST_DEV)
    owner_hits = (owner_blocks[:, :, None] == jnp.arange(N_BLK, dtype=jnp.int32)[None, None, :]).astype(jnp.int32)
    earlier = jnp.cumsum(owner_hits, axis=1) - owner_hits
    arrival = lax.optimization_barrier(jnp.sum(owner_hits * earlier, axis=2))
    slot_index = (jnp.arange(N_BLK, dtype=jnp.int32)[:, None] * CAP + arrival).reshape(-1).astype(jnp.int32)
    resident = jnp.zeros((N_BLK, RSLOTS, 2, BINS), jnp.bfloat16).at[owner_flat, slot_index].set(white_traces)
    bin_index = jnp.arange(BINS, dtype=jnp.int32)
    lag_value = (jnp.arange(OUT, dtype=jnp.int32) - OUT // 2) * DEC
    phase_angle = jnp.mod(bin_index[:, None] * lag_value[None, :], BINS).astype(jnp.float32) * (2.0 * math.pi / BINS)
    cosine_table = jnp.cos(phase_angle)
    sine_table = jnp.sin(phase_angle)
    norm_scale = BINS ** (-0.5)

    def per_block(block_index):
        chosen = lax.dynamic_slice_in_dim(white_sources, (block_index * VS).astype(jnp.int32), VS, 0).astype(jnp.float32)
        real_part = chosen[:, 0][:, :, None]
        imag_part = chosen[:, 1][:, :, None]
        kernel_real = (real_part * cosine_table[None] + imag_part * sine_table[None]) * norm_scale
        kernel_imag = (imag_part * cosine_table[None] - real_part * sine_table[None]) * norm_scale
        kernel = jnp.stack([kernel_real, kernel_imag], axis=1).astype(jnp.bfloat16)
        kernel = lax.optimization_barrier(kernel).astype(jnp.float32).reshape(VS, 2, N_BAND, GROUP_BINS, OUT)

        def per_offset(offset):
            visitor_index = jnp.mod(block_index - offset, N_BLK).astype(jnp.int32)
            visitor = lax.dynamic_index_in_dim(resident, visitor_index, 0, keepdims=False)
            visitor = visitor.astype(jnp.float32).reshape(RSLOTS, 2, N_BAND, GROUP_BINS)
            partial_value = jnp.einsum('rcgk,scgkl->gsrl', visitor, kernel)
            partial_value = lax.optimization_barrier(partial_value.astype(jnp.bfloat16)).astype(jnp.float32)
            return lax.optimization_barrier(jnp.sum(partial_value, axis=0))
        result = lax.map(per_offset, jnp.arange(Q, dtype=jnp.int32))
        return jnp.transpose(result, (1, 0, 2, 3))
    gathered = lax.map(per_block, jnp.arange(N_BLK, dtype=jnp.int32))
    return gathered.reshape(SOURCES, Q, RSLOTS, OUT)
```

```python
import math

import jax
import jax.numpy as jnp
from jax import lax
from jax.sharding import PartitionSpec as P

BINS = 8192
LAGS = 2048
DEC = 8
PERIOD = BINS // DEC


EPS = 1e-06


def per_device(traces, sources, owner):
    blocks = lax.axis_size("blk")
    station_count = traces.shape[0]
    source_count = sources.shape[0]
    group_bins = traces.shape[2]
    folds = group_bins // PERIOD
    capacity = max(2, 2 * station_count // blocks)
    lags_out = LAGS // DEC
    offsets = blocks // 4

    all_sources = lax.all_gather(sources, "blk", axis=0, tiled=True)

    trace_float = traces.astype(jnp.float32)
    all_source_float = all_sources.astype(jnp.float32)
    trace_power, source_power = lax.psum(
        (
            jnp.sum(trace_float * trace_float, axis=(1, 2)),
            jnp.sum(all_source_float * all_source_float, axis=(1, 2)),
        ),
        "band",
    )
    white_traces = (
        (trace_float * lax.rsqrt(trace_power / (2 * BINS) + EPS)[:, None, None])
        .astype(jnp.bfloat16)
        .reshape(station_count, 2 * group_bins)
    )
    white_sources = (
        (all_source_float * lax.rsqrt(source_power / (2 * BINS) + EPS)[:, None, None])
        .astype(jnp.bfloat16)
        .astype(jnp.float32)
        .reshape(blocks, source_count, 2, folds, PERIOD)
    )

    owners = owner[:, 0]
    owner_hits = (owners[:, None] == jnp.arange(blocks, dtype=jnp.int32)[None, :]).astype(jnp.int32)
    earlier = jnp.cumsum(owner_hits, axis=0) - owner_hits
    arrival = jnp.sum(owner_hits * earlier, axis=1)
    slot_index = owners * capacity + arrival
    placing = (
        jnp.arange(blocks * capacity, dtype=jnp.int32)[:, None] == slot_index[None, :]
    ).astype(jnp.bfloat16)
    placed = jnp.dot(placing, white_traces, preferred_element_type=jnp.float32)
    placed = placed.reshape(blocks, capacity, 2, folds, PERIOD)

    bin_index = jnp.arange(PERIOD, dtype=jnp.int32)
    lag_value = (jnp.arange(lags_out, dtype=jnp.int32) - lags_out // 2) * DEC
    phase_angle = jnp.mod(bin_index[:, None] * lag_value[None, :], BINS).astype(jnp.float32) * (
        2.0 * math.pi / BINS
    )
    table = jnp.concatenate([jnp.cos(phase_angle), jnp.sin(phase_angle)], axis=0).astype(
        jnp.bfloat16
    )
    norm_scale = BINS ** (-0.5)

    real_s = white_sources[:, None, :, 0]
    imag_s = white_sources[:, None, :, 1]
    cross = []
    for offset in range(offsets):
        visiting = jnp.roll(placed, offset, axis=0)
        real_t = visiting[:, :, None, 0]
        imag_t = visiting[:, :, None, 1]
        even = jnp.sum(real_t * real_s + imag_t * imag_s, axis=3)
        odd = jnp.sum(real_t * imag_s - imag_t * real_s, axis=3)
        cross.append(jnp.concatenate([even, odd], axis=-1))
    cross = jnp.stack(cross, axis=1).astype(jnp.bfloat16)
    rows = blocks * offsets * capacity * source_count
    partial = jnp.dot(
        cross.reshape(rows, 2 * PERIOD), table, preferred_element_type=jnp.float32
    )
    partial = (partial * norm_scale).astype(jnp.bfloat16)
    partial = partial.reshape(blocks, offsets, capacity, source_count, lags_out)
    arrived = lax.all_to_all(partial, "blk", split_axis=0, concat_axis=0, tiled=True)
    summed = lax.psum_scatter(
        arrived.astype(jnp.float32), "band", scatter_dimension=0, tiled=True
    )
    half = summed.shape[0]
    return jnp.transpose(summed, (3, 1, 0, 2, 4)).reshape(
        source_count, offsets, half * capacity, lags_out
    )


def solution(mesh):
    placed = (P("blk", None, "band"), P("blk", None, "band"), P("blk", None))
    return jax.shard_map(
        per_device,
        mesh=mesh,
        in_specs=placed,
        out_specs=P("blk", None, "band", None),
        check_vma=False,
    )
```

```python
import math

import jax
import jax.numpy as jnp
from jax import lax
from jax.sharding import PartitionSpec as P

BINS = 8192
LAGS = 2048
DEC = 8
PERIOD = BINS // DEC


EPS = 1e-06


def shifted(block, distance):
    count = lax.axis_size("blk")
    route = [(i, (i + distance) % count) for i in range(count)]
    return lax.ppermute(block, "blk", route)


def per_device(traces, sources, owner):
    blocks = lax.axis_size("blk")
    station_count = traces.shape[0]
    source_count = sources.shape[0]
    group_bins = traces.shape[2]
    folds = group_bins // PERIOD
    capacity = max(2, 2 * station_count // blocks)
    lags_out = LAGS // DEC
    offsets = blocks // 4
    me = lax.axis_index("blk")
    band = lax.axis_index("band")

    trace_float = traces.astype(jnp.float32)
    source_float = sources.astype(jnp.float32)
    trace_power, source_power = lax.psum(
        (
            jnp.sum(trace_float * trace_float, axis=(1, 2)),
            jnp.sum(source_float * source_float, axis=(1, 2)),
        ),
        "band",
    )
    white_sources = (
        source_float * lax.rsqrt(source_power / (2 * BINS) + EPS)[:, None, None]
    ).astype(jnp.bfloat16)
    visiting = jnp.stack(
        [white_sources] + [shifted(white_sources, j) for j in range(1, blocks)], axis=0
    )
    white_traces = (
        (trace_float * lax.rsqrt(trace_power / (2 * BINS) + EPS)[:, None, None])
        .astype(jnp.bfloat16)
        .reshape(station_count, 2 * group_bins)
    )

    owners = owner[:, 0]
    owner_hits = (owners[:, None] == jnp.arange(blocks, dtype=jnp.int32)[None, :]).astype(jnp.int32)
    earlier = jnp.cumsum(owner_hits, axis=0) - owner_hits
    arrival = jnp.sum(owner_hits * earlier, axis=1)
    slot_index = jnp.mod(me - owners, blocks) * capacity + arrival
    placing = (
        jnp.arange(blocks * capacity, dtype=jnp.int32)[:, None] == slot_index[None, :]
    ).astype(jnp.bfloat16)
    placed = jnp.dot(placing, white_traces, preferred_element_type=jnp.float32).astype(
        jnp.bfloat16
    )
    placed = placed.reshape(blocks, capacity, 2, folds, PERIOD)

    bin_index = jnp.arange(PERIOD, dtype=jnp.int32)
    lag_value = (jnp.arange(lags_out, dtype=jnp.int32) - lags_out // 2) * DEC
    phase_angle = jnp.mod(bin_index[:, None] * lag_value[None, :], BINS).astype(jnp.float32) * (
        2.0 * math.pi / BINS
    )
    table = jnp.concatenate([jnp.cos(phase_angle), jnp.sin(phase_angle)], axis=0).astype(
        jnp.bfloat16
    )
    norm_scale = BINS ** (-0.5)

    source_values = visiting.astype(jnp.float32).reshape(blocks, source_count, 2, folds, PERIOD)
    real_s = source_values[:, None, :, 0]
    imag_s = source_values[:, None, :, 1]
    cross = []
    for offset in range(offsets):
        owned = jnp.roll(placed, -offset, axis=0).astype(jnp.float32)
        real_t = owned[:, :, None, 0]
        imag_t = owned[:, :, None, 1]
        even = jnp.sum(real_t * real_s + imag_t * imag_s, axis=3)
        odd = jnp.sum(real_t * imag_s - imag_t * real_s, axis=3)
        cross.append(jnp.concatenate([even, odd], axis=-1))
    cross = jnp.stack(cross, axis=1).astype(jnp.bfloat16)
    rows = blocks * offsets * capacity * source_count
    partial = jnp.dot(
        cross.reshape(rows, 2 * PERIOD), table, preferred_element_type=jnp.float32
    )
    partial = (partial * norm_scale).astype(jnp.bfloat16)
    partial = partial.reshape(blocks, offsets, capacity, source_count, lags_out)
    returned = jnp.stack(
        [partial[0]] + [shifted(partial[j], blocks - j) for j in range(1, blocks)], axis=0
    )
    doubled = jnp.concatenate([returned, returned], axis=0)
    half = blocks // 2
    start = jnp.mod(-me, blocks)
    mine = lax.dynamic_slice_in_dim(doubled, start + band * half, half, axis=0)
    other = lax.dynamic_slice_in_dim(doubled, start + (1 - band) * half, half, axis=0)
    other = lax.ppermute(other, "band", [(0, 1), (1, 0)])
    summed = mine.astype(jnp.float32) + other.astype(jnp.float32)
    return jnp.transpose(summed, (3, 1, 0, 2, 4)).reshape(
        source_count, offsets, half * capacity, lags_out
    )


def solution(mesh):
    placed = (P("blk", None, "band"), P("blk", None, "band"), P("blk", None))
    return jax.shard_map(
        per_device,
        mesh=mesh,
        in_specs=placed,
        out_specs=P("blk", None, "band", None),
        check_vma=False,
    )
```

```python
import functools
import math

import jax
import jax.numpy as jnp
from jax import lax
from jax.experimental import pallas as pl
from jax.experimental.pallas import tpu as pltpu
from jax.sharding import PartitionSpec as P

BINS = 8192
LAGS = 2048
DEC = 8
PERIOD = BINS // DEC


EPS = 1e-06


def correlate_kernel(blocks, offsets, capacity, norm_scale, placed_ref, source_ref, table_ref, out_ref, cross_ref):
    block = pl.program_id(0)
    folds = placed_ref.shape[2] // PERIOD
    for offset in range(offsets):
        owned = placed_ref[lax.rem(block - offset + blocks, blocks)]
        real_t = owned[:capacity]
        imag_t = owned[capacity:]
        for source in range(2):
            real_s = source_ref[0, 2 * source : 2 * source + 1]
            imag_s = source_ref[0, 2 * source + 1 : 2 * source + 2]
            even = real_t * real_s + imag_t * imag_s
            odd = real_t * imag_s - imag_t * real_s
            even_fold = even[:, :PERIOD]
            odd_fold = odd[:, :PERIOD]
            for fold in range(1, folds):
                even_fold = even_fold + even[:, fold * PERIOD : (fold + 1) * PERIOD]
                odd_fold = odd_fold + odd[:, fold * PERIOD : (fold + 1) * PERIOD]
            row = (source * offsets + offset) * capacity
            cross_ref[row : row + capacity, :PERIOD] = even_fold
            cross_ref[row : row + capacity, PERIOD:] = odd_fold
    product = jnp.dot(
        cross_ref[...].astype(jnp.bfloat16), table_ref[...], preferred_element_type=jnp.float32
    )
    out_ref[0] = (product * norm_scale).astype(out_ref.dtype)


def correlate(placed, white_sources, table, offsets, capacity):
    blocks, _, group_bins = placed.shape
    rows = 2 * offsets * capacity
    lags_out = table.shape[1]
    body = functools.partial(correlate_kernel, blocks, offsets, capacity, BINS ** (-0.5))
    return pl.pallas_call(
        body,
        grid=(blocks,),
        in_specs=[
            pl.BlockSpec(placed.shape, lambda a: (0, 0, 0)),
            pl.BlockSpec((1,) + white_sources.shape[1:], lambda a: (a, 0, 0)),
            pl.BlockSpec(table.shape, lambda a: (0, 0)),
        ],
        out_specs=pl.BlockSpec((1, rows, lags_out), lambda a: (a, 0, 0)),
        out_shape=jax.ShapeDtypeStruct((blocks, rows, lags_out), jnp.bfloat16),
        scratch_shapes=[pltpu.VMEM((rows, 2 * PERIOD), jnp.float32)],
        cost_estimate=pl.CostEstimate(
            flops=blocks * rows * 2 * PERIOD * lags_out * 2 + blocks * offsets * 16 * capacity * group_bins,
            bytes_accessed=placed.size * 4 + white_sources.size * 4 + table.size * 2 + blocks * rows * lags_out * 2,
            transcendentals=0,
        ),
    )(placed, white_sources, table)


def per_device(traces, sources, owner):
    blocks = lax.axis_size("blk")
    band_count = lax.axis_size("band")
    station_count = traces.shape[0]
    source_count = sources.shape[0]
    group_bins = traces.shape[2]
    capacity = max(2, 2 * station_count // blocks)
    lags_out = LAGS // DEC
    offsets = blocks // 4
    band = lax.axis_index("band")

    every_source = lax.all_gather(sources, ("blk", "band"), axis=0, tiled=True)
    every_source = every_source.reshape(blocks, band_count, source_count, 2, group_bins)
    every_source = every_source.astype(jnp.float32)

    trace_float = traces.astype(jnp.float32)
    trace_power = lax.psum(jnp.sum(trace_float * trace_float, axis=(1, 2)), "band")
    white_traces = (
        (trace_float * lax.rsqrt(trace_power / (2 * BINS) + EPS)[:, None, None])
        .astype(jnp.bfloat16)
        .reshape(station_count, 2 * group_bins)
    )

    owners = owner[:, 0]
    owner_hits = (owners[:, None] == jnp.arange(blocks, dtype=jnp.int32)[None, :]).astype(jnp.int32)
    earlier = jnp.cumsum(owner_hits, axis=0) - owner_hits
    arrival = jnp.sum(owner_hits * earlier, axis=1)
    slot_index = owners * capacity + arrival
    placing = (
        jnp.arange(blocks * capacity, dtype=jnp.int32)[:, None] == slot_index[None, :]
    ).astype(jnp.bfloat16)
    placed = jnp.dot(placing, white_traces, preferred_element_type=jnp.float32)
    placed = placed.reshape(blocks, capacity, 2, group_bins).transpose(0, 2, 1, 3)
    placed = placed.reshape(blocks, 2 * capacity, group_bins)

    bin_index = jnp.arange(PERIOD, dtype=jnp.int32)
    lag_value = (jnp.arange(lags_out, dtype=jnp.int32) - lags_out // 2) * DEC
    phase_angle = jnp.mod(bin_index[:, None] * lag_value[None, :], BINS).astype(jnp.float32) * (
        2.0 * math.pi / BINS
    )
    table = jnp.concatenate([jnp.cos(phase_angle), jnp.sin(phase_angle)], axis=0).astype(
        jnp.bfloat16
    )

    source_power = jnp.sum(every_source * every_source, axis=(1, 3, 4))
    own_band = lax.dynamic_index_in_dim(every_source, band, axis=1, keepdims=False)
    white_sources = (
        (own_band * lax.rsqrt(source_power / (2 * BINS) + EPS)[:, :, None, None])
        .astype(jnp.bfloat16)
        .astype(jnp.float32)
        .reshape(blocks, source_count * 2, group_bins)
    )

    partial = correlate(placed, white_sources, table, offsets, capacity)
    arrived = lax.all_to_all(partial, "blk", split_axis=0, concat_axis=0, tiled=True)
    half = blocks // 2
    mine = lax.dynamic_slice_in_dim(arrived, band * half, half, axis=0)
    other = lax.dynamic_slice_in_dim(arrived, (1 - band) * half, half, axis=0)
    other = lax.ppermute(other, "band", [(0, 1), (1, 0)])
    summed = mine.astype(jnp.float32) + other.astype(jnp.float32)
    summed = summed.reshape(half, source_count, offsets, capacity, lags_out)
    return jnp.transpose(summed, (1, 2, 0, 3, 4)).reshape(
        source_count, offsets, half * capacity, lags_out
    )


def solution(mesh):
    placed = (P("blk", None, "band"), P("blk", None, "band"), P("blk", None))
    return jax.shard_map(
        per_device,
        mesh=mesh,
        in_specs=placed,
        out_specs=P("blk", None, "band", None),
        check_vma=False,
    )
```

```python
import functools
import math

import jax
import jax.numpy as jnp
from jax import lax
from jax.experimental import pallas as pl
from jax.experimental.pallas import tpu as pltpu
from jax.sharding import PartitionSpec as P

BINS = 8192
LAGS = 2048
DEC = 8
PERIOD = BINS // DEC


EPS = 1e-06


def correlate_kernel(blocks, offsets, capacity, norm_scale, placed_ref, source_ref, table_ref, out_ref, cross_ref):
    block = pl.program_id(0)
    folds = placed_ref.shape[2] // PERIOD
    for offset in range(offsets):
        owned = placed_ref[lax.rem(block - offset + blocks, blocks)]
        real_t = owned[:capacity]
        imag_t = owned[capacity:]
        for source in range(2):
            real_s = source_ref[0, 2 * source : 2 * source + 1]
            imag_s = source_ref[0, 2 * source + 1 : 2 * source + 2]
            even = real_t * real_s + imag_t * imag_s
            odd = real_t * imag_s - imag_t * real_s
            even_fold = even[:, :PERIOD]
            odd_fold = odd[:, :PERIOD]
            for fold in range(1, folds):
                even_fold = even_fold + even[:, fold * PERIOD : (fold + 1) * PERIOD]
                odd_fold = odd_fold + odd[:, fold * PERIOD : (fold + 1) * PERIOD]
            row = (source * offsets + offset) * capacity
            cross_ref[row : row + capacity, :PERIOD] = even_fold
            cross_ref[row : row + capacity, PERIOD:] = odd_fold
    product = jnp.dot(
        cross_ref[...].astype(jnp.bfloat16), table_ref[...], preferred_element_type=jnp.float32
    )
    out_ref[0] = (product * norm_scale).astype(out_ref.dtype)


def correlate(placed, white_sources, table, offsets, capacity):
    blocks, _, group_bins = placed.shape
    rows = 2 * offsets * capacity
    lags_out = table.shape[1]
    body = functools.partial(correlate_kernel, blocks, offsets, capacity, BINS ** (-0.5))
    return pl.pallas_call(
        body,
        grid=(blocks,),
        in_specs=[
            pl.BlockSpec(placed.shape, lambda a: (0, 0, 0)),
            pl.BlockSpec((1,) + white_sources.shape[1:], lambda a: (a, 0, 0)),
            pl.BlockSpec(table.shape, lambda a: (0, 0)),
        ],
        out_specs=pl.BlockSpec((1, rows, lags_out), lambda a: (a, 0, 0)),
        out_shape=jax.ShapeDtypeStruct((blocks, rows, lags_out), jnp.bfloat16),
        scratch_shapes=[pltpu.VMEM((rows, 2 * PERIOD), jnp.float32)],
        cost_estimate=pl.CostEstimate(
            flops=blocks * rows * 2 * PERIOD * lags_out * 2 + blocks * offsets * 16 * capacity * group_bins,
            bytes_accessed=placed.size * 4 + white_sources.size * 4 + table.size * 2 + blocks * rows * lags_out * 2,
            transcendentals=0,
        ),
    )(placed, white_sources, table)


def per_device(traces, sources, owner):
    blocks = lax.axis_size("blk")
    band_count = lax.axis_size("band")
    station_count = traces.shape[0]
    source_count = sources.shape[0]
    group_bins = traces.shape[2]
    capacity = max(2, 2 * station_count // blocks)
    lags_out = LAGS // DEC
    offsets = blocks // 4
    band = lax.axis_index("band")

    trace_float = traces.astype(jnp.float32)
    source_float = sources.astype(jnp.float32)
    trace_power, source_power = lax.psum(
        (
            jnp.sum(trace_float * trace_float, axis=(1, 2)),
            jnp.sum(source_float * source_float, axis=(1, 2)),
        ),
        "band",
    )
    white_sources = (
        source_float * lax.rsqrt(source_power / (2 * BINS) + EPS)[:, None, None]
    ).astype(jnp.bfloat16)
    me = lax.axis_index("blk")
    held = white_sources[None]
    step = 1
    while step < blocks:
        got = lax.ppermute(held, "blk", [(i, i ^ step) for i in range(blocks)])
        upper = jnp.bitwise_and(me // step, 1) == 1
        held = jnp.where(upper, jnp.concatenate([got, held]), jnp.concatenate([held, got]))
        step *= 2
    white_traces = (
        (trace_float * lax.rsqrt(trace_power / (2 * BINS) + EPS)[:, None, None])
        .astype(jnp.bfloat16)
        .reshape(station_count, 2 * group_bins)
    )

    owners = owner[:, 0]
    owner_hits = (owners[:, None] == jnp.arange(blocks, dtype=jnp.int32)[None, :]).astype(jnp.int32)
    earlier = jnp.cumsum(owner_hits, axis=0) - owner_hits
    arrival = jnp.sum(owner_hits * earlier, axis=1)
    slot_index = owners * capacity + arrival
    placing = (
        jnp.arange(blocks * capacity, dtype=jnp.int32)[:, None] == slot_index[None, :]
    ).astype(jnp.bfloat16)
    placed = jnp.dot(placing, white_traces, preferred_element_type=jnp.float32)
    placed = placed.reshape(blocks, capacity, 2, group_bins).transpose(0, 2, 1, 3)
    placed = placed.reshape(blocks, 2 * capacity, group_bins)

    bin_index = jnp.arange(PERIOD, dtype=jnp.int32)
    lag_value = (jnp.arange(lags_out, dtype=jnp.int32) - lags_out // 2) * DEC
    phase_angle = jnp.mod(bin_index[:, None] * lag_value[None, :], BINS).astype(jnp.float32) * (
        2.0 * math.pi / BINS
    )
    table = jnp.concatenate([jnp.cos(phase_angle), jnp.sin(phase_angle)], axis=0).astype(
        jnp.bfloat16
    )

    white_sources = held.astype(jnp.float32).reshape(blocks, source_count * 2, group_bins)

    partial = correlate(placed, white_sources, table, offsets, capacity)
    arrived = lax.all_to_all(partial, "blk", split_axis=0, concat_axis=0, tiled=True)
    half = blocks // 2
    mine = lax.dynamic_slice_in_dim(arrived, band * half, half, axis=0)
    other = lax.dynamic_slice_in_dim(arrived, (1 - band) * half, half, axis=0)
    other = lax.ppermute(other, "band", [(0, 1), (1, 0)])
    summed = mine.astype(jnp.float32) + other.astype(jnp.float32)
    summed = summed.reshape(half, source_count, offsets, capacity, lags_out)
    return jnp.transpose(summed, (1, 2, 0, 3, 4)).reshape(
        source_count, offsets, half * capacity, lags_out
    )


def solution(mesh):
    placed = (P("blk", None, "band"), P("blk", None, "band"), P("blk", None))
    return jax.shard_map(
        per_device,
        mesh=mesh,
        in_specs=placed,
        out_specs=P("blk", None, "band", None),
        check_vma=False,
    )
```

```python
import functools
import math

import jax
import ml_dtypes
import numpy as np
import jax.numpy as jnp
from jax import lax
from jax.experimental import pallas as pl
from jax.experimental.pallas import tpu as pltpu
from jax.sharding import PartitionSpec as P

BINS = 8192
LAGS = 2048
DEC = 8
PERIOD = BINS // DEC


EPS = 1e-06


def correlate_kernel(blocks, offsets, capacity, group, norm_scale, placed_ref, source_ref, table_ref, out_ref, cross_ref):
    first = pl.program_id(0) * group
    folds = placed_ref.shape[2] // PERIOD
    rows = 2 * offsets * capacity
    for member in range(group):
        block = first + member
        for offset in range(offsets):
            owned = placed_ref[lax.rem(block - offset + blocks, blocks)].astype(jnp.float32)
            real_t = owned[:capacity]
            imag_t = owned[capacity:]
            for source in range(2):
                real_s = source_ref[member, 2 * source : 2 * source + 1].astype(jnp.float32)
                imag_s = source_ref[member, 2 * source + 1 : 2 * source + 2].astype(jnp.float32)
                even = real_t * real_s + imag_t * imag_s
                odd = real_t * imag_s - imag_t * real_s
                even_fold = even[:, :PERIOD]
                odd_fold = odd[:, :PERIOD]
                for fold in range(1, folds):
                    even_fold = even_fold + even[:, fold * PERIOD : (fold + 1) * PERIOD]
                    odd_fold = odd_fold + odd[:, fold * PERIOD : (fold + 1) * PERIOD]
                row = member * rows + (source * offsets + offset) * capacity
                cross_ref[row : row + capacity, :PERIOD] = even_fold
                cross_ref[row : row + capacity, PERIOD:] = odd_fold
    product = jnp.dot(
        cross_ref[...].astype(jnp.bfloat16), table_ref[...], preferred_element_type=jnp.float32
    )
    product = (product * norm_scale).astype(out_ref.dtype)
    for member in range(group):
        out_ref[member] = product[member * rows : (member + 1) * rows]


def correlate(placed, white_sources, table, offsets, capacity):
    blocks, _, group_bins = placed.shape
    rows = 2 * offsets * capacity
    lags_out = table.shape[1]
    group = 4
    body = functools.partial(correlate_kernel, blocks, offsets, capacity, group, BINS ** (-0.5))
    return pl.pallas_call(
        body,
        grid=(blocks // group,),
        in_specs=[
            pl.BlockSpec(placed.shape, lambda a: (0, 0, 0)),
            pl.BlockSpec((group,) + white_sources.shape[1:], lambda a: (a, 0, 0)),
            pl.BlockSpec(table.shape, lambda a: (0, 0)),
        ],
        out_specs=pl.BlockSpec((group, rows, lags_out), lambda a: (a, 0, 0)),
        out_shape=jax.ShapeDtypeStruct((blocks, rows, lags_out), jnp.bfloat16),
        scratch_shapes=[pltpu.VMEM((group * rows, 2 * PERIOD), jnp.float32)],
        cost_estimate=pl.CostEstimate(
            flops=blocks * rows * 2 * PERIOD * lags_out * 2 + blocks * offsets * 16 * capacity * group_bins,
            bytes_accessed=placed.size * 2 + white_sources.size * 2 + table.size * 2 + blocks * rows * lags_out * 2,
            transcendentals=0,
        ),
    )(placed, white_sources, table)


def twiddle_table(lags_out):
    bin_index = np.arange(PERIOD, dtype=np.int64)
    lag_value = (np.arange(lags_out, dtype=np.int64) - lags_out // 2) * DEC
    phase = np.mod(bin_index[:, None] * lag_value[None, :], BINS).astype(np.float32)
    phase = (phase * np.float32(2.0 * math.pi / BINS)).astype(np.float64)
    table = np.concatenate([np.cos(phase), np.sin(phase)], axis=0)
    return table.astype(ml_dtypes.bfloat16)


def per_device(traces, sources, owner):
    blocks = lax.axis_size("blk")
    band_count = lax.axis_size("band")
    station_count = traces.shape[0]
    source_count = sources.shape[0]
    group_bins = traces.shape[2]
    capacity = max(2, 2 * station_count // blocks)
    lags_out = LAGS // DEC
    offsets = blocks // 4
    band = lax.axis_index("band")

    trace_float = traces.astype(jnp.float32)
    source_float = sources.astype(jnp.float32)
    trace_power, source_power = lax.psum(
        (
            jnp.sum(trace_float * trace_float, axis=(1, 2)),
            jnp.sum(source_float * source_float, axis=(1, 2)),
        ),
        "band",
    )
    white_sources = (
        source_float * lax.rsqrt(source_power / (2 * BINS) + EPS)[:, None, None]
    ).astype(jnp.bfloat16)
    me = lax.axis_index("blk")
    held = white_sources[None]
    bits = blocks.bit_length() - 1
    for bit in reversed(range(bits)):
        step = 1 << bit
        got = lax.ppermute(held, "blk", [(i, i ^ step) for i in range(blocks)])
        upper = jnp.bitwise_and(me // step, 1) == 1
        held = jnp.where(upper, jnp.concatenate([got, held]), jnp.concatenate([held, got]))
    held = held.reshape((2,) * bits + held.shape[1:])
    held = held.transpose(tuple(reversed(range(bits))) + tuple(range(bits, held.ndim)))
    white_traces = (
        (trace_float * lax.rsqrt(trace_power / (2 * BINS) + EPS)[:, None, None])
        .astype(jnp.bfloat16)
        .reshape(station_count, 2 * group_bins)
    )

    owners = owner[:, 0]
    owner_hits = (owners[:, None] == jnp.arange(blocks, dtype=jnp.int32)[None, :]).astype(jnp.int32)
    earlier = jnp.cumsum(owner_hits, axis=0) - owner_hits
    arrival = jnp.sum(owner_hits * earlier, axis=1)
    slot_index = owners * capacity + arrival
    placing = (
        jnp.arange(blocks * capacity, dtype=jnp.int32)[:, None] == slot_index[None, :]
    ).astype(jnp.bfloat16)
    placed = jnp.dot(placing, white_traces, preferred_element_type=jnp.float32).astype(jnp.bfloat16)
    placed = placed.reshape(blocks, capacity, 2, group_bins).transpose(0, 2, 1, 3)
    placed = placed.reshape(blocks, 2 * capacity, group_bins)

    table = jnp.asarray(twiddle_table(lags_out))

    white_sources = held.reshape(blocks, source_count * 2, group_bins)

    partial = correlate(placed, white_sources, table, offsets, capacity)
    arrived = lax.all_to_all(partial, "blk", split_axis=0, concat_axis=0, tiled=True)
    half = blocks // 2
    mine = lax.dynamic_slice_in_dim(arrived, band * half, half, axis=0)
    other = lax.dynamic_slice_in_dim(arrived, (1 - band) * half, half, axis=0)
    other = lax.ppermute(other, "band", [(0, 1), (1, 0)])
    summed = mine.astype(jnp.float32) + other.astype(jnp.float32)
    summed = summed.reshape(half, source_count, offsets, capacity, lags_out)
    return jnp.transpose(summed, (1, 2, 0, 3, 4)).reshape(
        source_count, offsets, half * capacity, lags_out
    )


def solution(mesh):
    placed = (P("blk", None, "band"), P("blk", None, "band"), P("blk", None))
    return jax.shard_map(
        per_device,
        mesh=mesh,
        in_specs=placed,
        out_specs=P("blk", None, "band", None),
        check_vma=False,
    )
```

```python
import functools
import math

import jax
import ml_dtypes
import numpy as np
import jax.numpy as jnp
from jax import lax
from jax.experimental import pallas as pl
from jax.experimental.pallas import tpu as pltpu
from jax.sharding import PartitionSpec as P

BINS = 8192
LAGS = 2048
DEC = 8
PERIOD = BINS // DEC


EPS = 1e-06


def correlate_kernel(blocks, offsets, capacity, group, norm_scale, ids_ref, placed_ref, source_ref, table_ref, out_ref, cross_ref):
    first = pl.program_id(0) * group
    folds = placed_ref.shape[2] // PERIOD
    rows = 2 * offsets * capacity
    for member in range(group):
        block = ids_ref[first + member]
        for source in range(2):
            real_s = source_ref[member, 2 * source : 2 * source + 1].astype(jnp.float32)
            imag_s = source_ref[member, 2 * source + 1 : 2 * source + 2].astype(jnp.float32)
            real_s = jnp.broadcast_to(real_s, (capacity, real_s.shape[1]))
            imag_s = jnp.broadcast_to(imag_s, (capacity, imag_s.shape[1]))
            for offset in range(offsets):
                owned = placed_ref[lax.rem(block - offset + blocks, blocks)].astype(jnp.float32)
                real_t = owned[:capacity]
                imag_t = owned[capacity:]
                even = real_t * real_s + imag_t * imag_s
                odd = real_t * imag_s - imag_t * real_s
                even_fold = even[:, :PERIOD]
                odd_fold = odd[:, :PERIOD]
                for fold in range(1, folds):
                    even_fold = even_fold + even[:, fold * PERIOD : (fold + 1) * PERIOD]
                    odd_fold = odd_fold + odd[:, fold * PERIOD : (fold + 1) * PERIOD]
                row = member * rows + (source * offsets + offset) * capacity
                cross_ref[row : row + capacity, :PERIOD] = even_fold
                cross_ref[row : row + capacity, PERIOD:] = odd_fold
    product = jnp.dot(
        cross_ref[...].astype(jnp.bfloat16), table_ref[...], preferred_element_type=jnp.float32
    )
    product = (product * norm_scale).astype(out_ref.dtype)
    for member in range(group):
        out_ref[member] = product[member * rows : (member + 1) * rows]


def correlate(ids, placed, white_sources, table, offsets, capacity):
    blocks, _, group_bins = placed.shape
    count = white_sources.shape[0]
    rows = 2 * offsets * capacity
    lags_out = table.shape[1]
    group = min(4, count)
    body = functools.partial(correlate_kernel, blocks, offsets, capacity, group, BINS ** (-0.5))
    return pl.pallas_call(
        body,
        grid_spec=pltpu.PrefetchScalarGridSpec(
            num_scalar_prefetch=1,
            grid=(count // group,),
            in_specs=[
                pl.BlockSpec(placed.shape, lambda a, ids: (0, 0, 0)),
                pl.BlockSpec((group,) + white_sources.shape[1:], lambda a, ids: (a, 0, 0)),
                pl.BlockSpec(table.shape, lambda a, ids: (0, 0)),
            ],
            out_specs=pl.BlockSpec((group, rows, lags_out), lambda a, ids: (a, 0, 0)),
            scratch_shapes=[pltpu.VMEM((group * rows, 2 * PERIOD), jnp.float32)],
        ),
        out_shape=jax.ShapeDtypeStruct((count, rows, lags_out), jnp.bfloat16),
        cost_estimate=pl.CostEstimate(
            flops=count * rows * 2 * PERIOD * lags_out * 2 + count * offsets * 16 * capacity * group_bins,
            bytes_accessed=placed.size * 2 + white_sources.size * 2 + table.size * 2 + count * rows * lags_out * 2,
            transcendentals=0,
        ),
    )(ids, placed, white_sources, table)


def twiddle_table(lags_out):
    bin_index = np.arange(PERIOD, dtype=np.int64)
    lag_value = (np.arange(lags_out, dtype=np.int64) - lags_out // 2) * DEC
    phase = np.mod(bin_index[:, None] * lag_value[None, :], BINS).astype(np.float32)
    phase = (phase * np.float32(2.0 * math.pi / BINS)).astype(np.float64)
    table = np.concatenate([np.cos(phase), np.sin(phase)], axis=0)
    return table.astype(ml_dtypes.bfloat16)


def per_device(traces, sources, owner):
    blocks = lax.axis_size("blk")
    band_count = lax.axis_size("band")
    station_count = traces.shape[0]
    source_count = sources.shape[0]
    group_bins = traces.shape[2]
    capacity = max(2, 2 * station_count // blocks)
    lags_out = LAGS // DEC
    offsets = blocks // 4
    band = lax.axis_index("band")

    source_float = sources.astype(jnp.float32)
    source_power = lax.psum(jnp.sum(source_float * source_float, axis=(1, 2)), "band")
    white_sources = (
        source_float * lax.rsqrt(source_power / (2 * BINS) + EPS)[:, None, None]
    ).astype(jnp.bfloat16).reshape(1, source_count * 2, group_bins)
    trace_float = traces.astype(jnp.float32)
    trace_power = lax.psum(jnp.sum(trace_float * trace_float, axis=(1, 2)), "band")
    white_traces = (
        (trace_float * lax.rsqrt(trace_power / (2 * BINS) + EPS)[:, None, None])
        .astype(jnp.bfloat16)
        .reshape(station_count, 2 * group_bins)
    )

    owners = owner[:, 0]
    owner_hits = (owners[:, None] == jnp.arange(blocks, dtype=jnp.int32)[None, :]).astype(jnp.int32)
    earlier = jnp.cumsum(owner_hits, axis=0) - owner_hits
    arrival = jnp.sum(owner_hits * earlier, axis=1)
    slot_index = owners * capacity + arrival
    placing = (
        jnp.arange(blocks * capacity, dtype=jnp.int32)[:, None] == slot_index[None, :]
    ).astype(jnp.bfloat16)
    placed = jnp.dot(placing, white_traces, preferred_element_type=jnp.float32).astype(jnp.bfloat16)
    placed = placed.reshape(blocks, capacity, 2, group_bins).transpose(0, 2, 1, 3)
    placed = placed.reshape(blocks, 2 * capacity, group_bins)

    table = jnp.asarray(twiddle_table(lags_out))

    me = lax.axis_index("blk")
    held = white_sources
    held_ids = me[None].astype(jnp.int32)
    results = correlate(held_ids, placed, held, table, offsets, capacity)
    bits = blocks.bit_length() - 1
    for bit in reversed(range(bits)):
        step = 1 << bit
        got = lax.ppermute(held, "blk", [(i, i ^ step) for i in range(blocks)])
        got_ids = jnp.bitwise_xor(held_ids, step)
        got_results = correlate(got_ids, placed, got, table, offsets, capacity)
        upper = jnp.bitwise_and(me // step, 1) == 1
        if bit > 0:
            held = jnp.where(upper, jnp.concatenate([got, held]), jnp.concatenate([held, got]))
            held_ids = jnp.where(upper, jnp.concatenate([got_ids, held_ids]), jnp.concatenate([held_ids, got_ids]))
        results = jnp.where(
            upper, jnp.concatenate([got_results, results]), jnp.concatenate([results, got_results])
        )
    partial = results.reshape((2,) * bits + results.shape[1:])
    partial = partial.transpose(tuple(reversed(range(bits))) + tuple(range(bits, partial.ndim)))
    partial = partial.reshape(results.shape)
    arrived = lax.all_to_all(partial, "blk", split_axis=0, concat_axis=0, tiled=True)
    half = blocks // 2
    mine = lax.dynamic_slice_in_dim(arrived, band * half, half, axis=0)
    other = lax.dynamic_slice_in_dim(arrived, (1 - band) * half, half, axis=0)
    other = lax.ppermute(other, "band", [(0, 1), (1, 0)])
    summed = mine.astype(jnp.float32) + other.astype(jnp.float32)
    summed = summed.reshape(half, source_count, offsets, capacity, lags_out)
    return jnp.transpose(summed, (1, 2, 0, 3, 4)).reshape(
        source_count, offsets, half * capacity, lags_out
    )


def solution(mesh):
    placed = (P("blk", None, "band"), P("blk", None, "band"), P("blk", None))
    return jax.shard_map(
        per_device,
        mesh=mesh,
        in_specs=placed,
        out_specs=P("blk", None, "band", None),
        check_vma=False,
    )
```

```python
import functools
import math

import jax
import ml_dtypes
import numpy as np
import jax.numpy as jnp
from jax import lax
from jax.experimental import pallas as pl
from jax.experimental.pallas import tpu as pltpu
from jax.sharding import PartitionSpec as P

BINS = 8192
LAGS = 2048
DEC = 8
PERIOD = BINS // DEC


EPS = 1e-06


def correlate_kernel(blocks, offsets, capacity, group, norm_scale, placed_ref, source_ref, table_ref, out_ref, cross_ref):
    first = pl.program_id(0) * group
    folds = placed_ref.shape[2] // PERIOD
    rows = 2 * offsets * capacity
    for member in range(group):
        block = first + member
        for offset in range(offsets):
            owned = placed_ref[lax.rem(block - offset + blocks, blocks)].astype(jnp.float32)
            real_t = owned[:capacity]
            imag_t = owned[capacity:]
            for source in range(2):
                real_s = source_ref[member, 2 * source : 2 * source + 1].astype(jnp.float32)
                imag_s = source_ref[member, 2 * source + 1 : 2 * source + 2].astype(jnp.float32)
                even = real_t * real_s + imag_t * imag_s
                odd = real_t * imag_s - imag_t * real_s
                even_fold = even[:, :PERIOD]
                odd_fold = odd[:, :PERIOD]
                for fold in range(1, folds):
                    even_fold = even_fold + even[:, fold * PERIOD : (fold + 1) * PERIOD]
                    odd_fold = odd_fold + odd[:, fold * PERIOD : (fold + 1) * PERIOD]
                row = member * rows + (source * offsets + offset) * capacity
                cross_ref[row : row + capacity, :PERIOD] = even_fold
                cross_ref[row : row + capacity, PERIOD:] = odd_fold
    product = jnp.dot(
        cross_ref[...].astype(jnp.bfloat16), table_ref[...], preferred_element_type=jnp.float32
    )
    product = (product * norm_scale).astype(out_ref.dtype)
    for member in range(group):
        out_ref[member] = product[member * rows : (member + 1) * rows]


def correlate(placed, white_sources, table, offsets, capacity):
    blocks, _, group_bins = placed.shape
    rows = 2 * offsets * capacity
    lags_out = table.shape[1]
    group = 4
    body = functools.partial(correlate_kernel, blocks, offsets, capacity, group, BINS ** (-0.5))
    return pl.pallas_call(
        body,
        grid=(blocks // group,),
        in_specs=[
            pl.BlockSpec(placed.shape, lambda a: (0, 0, 0)),
            pl.BlockSpec((group,) + white_sources.shape[1:], lambda a: (a, 0, 0)),
            pl.BlockSpec(table.shape, lambda a: (0, 0)),
        ],
        out_specs=pl.BlockSpec((group, rows, lags_out), lambda a: (a, 0, 0)),
        out_shape=jax.ShapeDtypeStruct((blocks, rows, lags_out), jnp.bfloat16),
        scratch_shapes=[pltpu.VMEM((group * rows, 2 * PERIOD), jnp.float32)],
        cost_estimate=pl.CostEstimate(
            flops=blocks * rows * 2 * PERIOD * lags_out * 2 + blocks * offsets * 16 * capacity * group_bins,
            bytes_accessed=placed.size * 2 + white_sources.size * 2 + table.size * 2 + blocks * rows * lags_out * 2,
            transcendentals=0,
        ),
    )(placed, white_sources, table)


def twiddle_table(lags_out):
    bin_index = np.arange(PERIOD, dtype=np.int64)
    lag_value = (np.arange(lags_out, dtype=np.int64) - lags_out // 2) * DEC
    phase = np.mod(bin_index[:, None] * lag_value[None, :], BINS).astype(np.float32)
    phase = (phase * np.float32(2.0 * math.pi / BINS)).astype(np.float64)
    table = np.concatenate([np.cos(phase), np.sin(phase)], axis=0)
    return table.astype(ml_dtypes.bfloat16)


def per_device(traces, sources, owner):
    blocks = lax.axis_size("blk")
    band_count = lax.axis_size("band")
    station_count = traces.shape[0]
    source_count = sources.shape[0]
    group_bins = traces.shape[2]
    capacity = max(2, 2 * station_count // blocks)
    lags_out = LAGS // DEC
    offsets = blocks // 4
    band = lax.axis_index("band")

    source_float = sources.astype(jnp.float32)
    source_sums = jnp.sum(source_float * source_float, axis=(1, 2))
    source_power = source_sums + lax.ppermute(source_sums, "band", [(0, 1), (1, 0)])
    trace_float = traces.astype(jnp.float32)
    trace_power = lax.psum(jnp.sum(trace_float * trace_float, axis=(1, 2)), "band")
    white_sources = (
        source_float * lax.rsqrt(source_power / (2 * BINS) + EPS)[:, None, None]
    ).astype(jnp.bfloat16)
    me = lax.axis_index("blk")
    held = white_sources[None]
    bits = blocks.bit_length() - 1
    for bit in reversed(range(bits)):
        step = 1 << bit
        got = lax.ppermute(held, "blk", [(i, i ^ step) for i in range(blocks)])
        upper = jnp.bitwise_and(me // step, 1) == 1
        held = jnp.where(upper, jnp.concatenate([got, held]), jnp.concatenate([held, got]))
    held = held.reshape((2,) * bits + held.shape[1:])
    held = held.transpose(tuple(reversed(range(bits))) + tuple(range(bits, held.ndim)))
    white_traces = (
        (trace_float * lax.rsqrt(trace_power / (2 * BINS) + EPS)[:, None, None])
        .astype(jnp.bfloat16)
        .reshape(station_count, 2 * group_bins)
    )

    owners = owner[:, 0]
    owner_hits = (owners[:, None] == jnp.arange(blocks, dtype=jnp.int32)[None, :]).astype(jnp.int32)
    earlier = jnp.cumsum(owner_hits, axis=0) - owner_hits
    arrival = jnp.sum(owner_hits * earlier, axis=1)
    slot_index = owners * capacity + arrival
    placing = (
        jnp.arange(blocks * capacity, dtype=jnp.int32)[:, None] == slot_index[None, :]
    ).astype(jnp.bfloat16)
    placed = jnp.dot(placing, white_traces, preferred_element_type=jnp.float32).astype(jnp.bfloat16)
    placed = placed.reshape(blocks, capacity, 2, group_bins).transpose(0, 2, 1, 3)
    placed = placed.reshape(blocks, 2 * capacity, group_bins)

    table = jnp.asarray(twiddle_table(lags_out))

    white_sources = held.reshape(blocks, source_count * 2, group_bins)

    partial = correlate(placed, white_sources, table, offsets, capacity)
    arrived = lax.all_to_all(partial, "blk", split_axis=0, concat_axis=0, tiled=True)
    half = blocks // 2
    mine = lax.dynamic_slice_in_dim(arrived, band * half, half, axis=0)
    other = lax.dynamic_slice_in_dim(arrived, (1 - band) * half, half, axis=0)
    other = lax.ppermute(other, "band", [(0, 1), (1, 0)])
    summed = mine.astype(jnp.float32) + other.astype(jnp.float32)
    summed = summed.reshape(half, source_count, offsets, capacity, lags_out)
    return jnp.transpose(summed, (1, 2, 0, 3, 4)).reshape(
        source_count, offsets, half * capacity, lags_out
    )


def solution(mesh):
    placed = (P("blk", None, "band"), P("blk", None, "band"), P("blk", None))
    return jax.shard_map(
        per_device,
        mesh=mesh,
        in_specs=placed,
        out_specs=P("blk", None, "band", None),
        check_vma=False,
    )
```

```python
import functools
import math

import jax
import ml_dtypes
import numpy as np
import jax.numpy as jnp
from jax import lax
from jax.experimental import pallas as pl
from jax.experimental.pallas import tpu as pltpu
from jax.sharding import PartitionSpec as P

BINS = 8192
LAGS = 2048
DEC = 8
PERIOD = BINS // DEC


EPS = 1e-06


def correlate_kernel(blocks, offsets, capacity, group, norm_scale, counts_ref, placed_ref, source_ref, table_ref, out_ref, cross_ref):
    first = pl.program_id(0) * group
    folds = placed_ref.shape[2] // PERIOD
    rows = 2 * offsets * capacity
    for member in range(group):
        block = first + member
        for offset in range(offsets):
            owner_block = lax.rem(block - offset + blocks, blocks)
            occupied = counts_ref[owner_block] > 0

            @pl.when(occupied)
            def _():
                owned = placed_ref[owner_block].astype(jnp.float32)
                real_t = owned[:capacity]
                imag_t = owned[capacity:]
                for source in range(2):
                    real_s = source_ref[member, 2 * source : 2 * source + 1].astype(jnp.float32)
                    imag_s = source_ref[member, 2 * source + 1 : 2 * source + 2].astype(jnp.float32)
                    even = real_t * real_s + imag_t * imag_s
                    odd = real_t * imag_s - imag_t * real_s
                    even_fold = even[:, :PERIOD]
                    odd_fold = odd[:, :PERIOD]
                    for fold in range(1, folds):
                        even_fold = even_fold + even[:, fold * PERIOD : (fold + 1) * PERIOD]
                        odd_fold = odd_fold + odd[:, fold * PERIOD : (fold + 1) * PERIOD]
                    row = member * rows + (source * offsets + offset) * capacity
                    cross_ref[row : row + capacity, :PERIOD] = even_fold
                    cross_ref[row : row + capacity, PERIOD:] = odd_fold

            @pl.when(jnp.logical_not(occupied))
            def _():
                for source in range(2):
                    row = member * rows + (source * offsets + offset) * capacity
                    cross_ref[row : row + capacity, :] = jnp.zeros((capacity, 2 * PERIOD), jnp.float32)

    product = jnp.dot(
        cross_ref[...].astype(jnp.bfloat16), table_ref[...], preferred_element_type=jnp.float32
    )
    product = (product * norm_scale).astype(out_ref.dtype)
    for member in range(group):
        out_ref[member] = product[member * rows : (member + 1) * rows]


def correlate(counts, placed, white_sources, table, offsets, capacity):
    blocks, _, group_bins = placed.shape
    rows = 2 * offsets * capacity
    lags_out = table.shape[1]
    group = 4
    body = functools.partial(correlate_kernel, blocks, offsets, capacity, group, BINS ** (-0.5))
    return pl.pallas_call(
        body,
        grid_spec=pltpu.PrefetchScalarGridSpec(
            num_scalar_prefetch=1,
            grid=(blocks // group,),
            in_specs=[
                pl.BlockSpec(placed.shape, lambda a, counts: (0, 0, 0)),
                pl.BlockSpec((group,) + white_sources.shape[1:], lambda a, counts: (a, 0, 0)),
                pl.BlockSpec(table.shape, lambda a, counts: (0, 0)),
            ],
            out_specs=pl.BlockSpec((group, rows, lags_out), lambda a, counts: (a, 0, 0)),
            scratch_shapes=[pltpu.VMEM((group * rows, 2 * PERIOD), jnp.float32)],
        ),
        out_shape=jax.ShapeDtypeStruct((blocks, rows, lags_out), jnp.bfloat16),
        cost_estimate=pl.CostEstimate(
            flops=blocks * rows * 2 * PERIOD * lags_out * 2 + blocks * offsets * 16 * capacity * group_bins,
            bytes_accessed=placed.size * 2 + white_sources.size * 2 + table.size * 2 + blocks * rows * lags_out * 2,
            transcendentals=0,
        ),
    )(counts, placed, white_sources, table)


def twiddle_table(lags_out):
    bin_index = np.arange(PERIOD, dtype=np.int64)
    lag_value = (np.arange(lags_out, dtype=np.int64) - lags_out // 2) * DEC
    phase = np.mod(bin_index[:, None] * lag_value[None, :], BINS).astype(np.float32)
    phase = (phase * np.float32(2.0 * math.pi / BINS)).astype(np.float64)
    table = np.concatenate([np.cos(phase), np.sin(phase)], axis=0)
    return table.astype(ml_dtypes.bfloat16)


def per_device(traces, sources, owner):
    blocks = lax.axis_size("blk")
    band_count = lax.axis_size("band")
    station_count = traces.shape[0]
    source_count = sources.shape[0]
    group_bins = traces.shape[2]
    capacity = max(2, 2 * station_count // blocks)
    lags_out = LAGS // DEC
    offsets = blocks // 4
    band = lax.axis_index("band")

    trace_float = traces.astype(jnp.float32)
    source_float = sources.astype(jnp.float32)
    trace_power, source_power = lax.psum(
        (
            jnp.sum(trace_float * trace_float, axis=(1, 2)),
            jnp.sum(source_float * source_float, axis=(1, 2)),
        ),
        "band",
    )
    white_sources = (
        source_float * lax.rsqrt(source_power / (2 * BINS) + EPS)[:, None, None]
    ).astype(jnp.bfloat16)
    me = lax.axis_index("blk")
    held = white_sources[None]
    bits = blocks.bit_length() - 1
    for bit in reversed(range(bits)):
        step = 1 << bit
        got = lax.ppermute(held, "blk", [(i, i ^ step) for i in range(blocks)])
        upper = jnp.bitwise_and(me // step, 1) == 1
        held = jnp.where(upper, jnp.concatenate([got, held]), jnp.concatenate([held, got]))
    held = held.reshape((2,) * bits + held.shape[1:])
    held = held.transpose(tuple(reversed(range(bits))) + tuple(range(bits, held.ndim)))
    white_traces = (
        (trace_float * lax.rsqrt(trace_power / (2 * BINS) + EPS)[:, None, None])
        .astype(jnp.bfloat16)
        .reshape(station_count, 2 * group_bins)
    )

    owners = owner[:, 0]
    owner_hits = (owners[:, None] == jnp.arange(blocks, dtype=jnp.int32)[None, :]).astype(jnp.int32)
    earlier = jnp.cumsum(owner_hits, axis=0) - owner_hits
    arrival = jnp.sum(owner_hits * earlier, axis=1)
    slot_index = owners * capacity + arrival
    placing = (
        jnp.arange(blocks * capacity, dtype=jnp.int32)[:, None] == slot_index[None, :]
    ).astype(jnp.bfloat16)
    placed = jnp.dot(placing, white_traces, preferred_element_type=jnp.float32).astype(jnp.bfloat16)
    placed = placed.reshape(blocks, capacity, 2, group_bins).transpose(0, 2, 1, 3)
    placed = placed.reshape(blocks, 2 * capacity, group_bins)

    table = jnp.asarray(twiddle_table(lags_out))

    white_sources = held.reshape(blocks, source_count * 2, group_bins)

    counts = jnp.sum(owner_hits, axis=0).astype(jnp.int32)
    partial = correlate(counts, placed, white_sources, table, offsets, capacity)
    arrived = lax.all_to_all(partial, "blk", split_axis=0, concat_axis=0, tiled=True)
    half = blocks // 2
    mine = lax.dynamic_slice_in_dim(arrived, band * half, half, axis=0)
    other = lax.dynamic_slice_in_dim(arrived, (1 - band) * half, half, axis=0)
    other = lax.ppermute(other, "band", [(0, 1), (1, 0)])
    summed = mine.astype(jnp.float32) + other.astype(jnp.float32)
    summed = summed.reshape(half, source_count, offsets, capacity, lags_out)
    return jnp.transpose(summed, (1, 2, 0, 3, 4)).reshape(
        source_count, offsets, half * capacity, lags_out
    )


def solution(mesh):
    placed = (P("blk", None, "band"), P("blk", None, "band"), P("blk", None))
    return jax.shard_map(
        per_device,
        mesh=mesh,
        in_specs=placed,
        out_specs=P("blk", None, "band", None),
        check_vma=False,
    )
```

```python
import functools
import math

import jax
import ml_dtypes
import numpy as np
import jax.numpy as jnp
from jax import lax
from jax.experimental import pallas as pl
from jax.experimental.pallas import tpu as pltpu
from jax.sharding import PartitionSpec as P

BINS = 8192
LAGS = 2048
DEC = 8
PERIOD = BINS // DEC


EPS = 1e-06


def correlate_kernel(blocks, offsets, capacity, group, norm_scale, ids_ref, placed_ref, source_ref, table_ref, out_ref, cross_ref):
    first = pl.program_id(0) * group
    folds = placed_ref.shape[2] // PERIOD
    rows = 2 * offsets * capacity
    for member in range(group):
        block = ids_ref[first + member]
        for offset in range(offsets):
            owned = placed_ref[lax.rem(block - offset + blocks, blocks)].astype(jnp.float32)
            real_t = owned[:capacity]
            imag_t = owned[capacity:]
            for source in range(2):
                real_s = source_ref[member, 2 * source : 2 * source + 1].astype(jnp.float32)
                imag_s = source_ref[member, 2 * source + 1 : 2 * source + 2].astype(jnp.float32)
                even = real_t * real_s + imag_t * imag_s
                odd = real_t * imag_s - imag_t * real_s
                even_fold = even[:, :PERIOD]
                odd_fold = odd[:, :PERIOD]
                for fold in range(1, folds):
                    even_fold = even_fold + even[:, fold * PERIOD : (fold + 1) * PERIOD]
                    odd_fold = odd_fold + odd[:, fold * PERIOD : (fold + 1) * PERIOD]
                row = member * rows + (source * offsets + offset) * capacity
                cross_ref[row : row + capacity, :PERIOD] = even_fold
                cross_ref[row : row + capacity, PERIOD:] = odd_fold
    product = jnp.dot(
        cross_ref[...].astype(jnp.bfloat16), table_ref[...], preferred_element_type=jnp.float32
    )
    product = (product * norm_scale).astype(out_ref.dtype)
    for member in range(group):
        out_ref[member] = product[member * rows : (member + 1) * rows]


def correlate(ids, placed, white_sources, table, offsets, capacity):
    blocks, _, group_bins = placed.shape
    count = white_sources.shape[0]
    rows = 2 * offsets * capacity
    lags_out = table.shape[1]
    group = min(4, count)
    body = functools.partial(correlate_kernel, blocks, offsets, capacity, group, BINS ** (-0.5))
    return pl.pallas_call(
        body,
        grid_spec=pltpu.PrefetchScalarGridSpec(
            num_scalar_prefetch=1,
            grid=(count // group,),
            in_specs=[
                pl.BlockSpec(placed.shape, lambda a, ids: (0, 0, 0)),
                pl.BlockSpec((group,) + white_sources.shape[1:], lambda a, ids: (a, 0, 0)),
                pl.BlockSpec(table.shape, lambda a, ids: (0, 0)),
            ],
            out_specs=pl.BlockSpec((group, rows, lags_out), lambda a, ids: (a, 0, 0)),
            scratch_shapes=[pltpu.VMEM((group * rows, 2 * PERIOD), jnp.float32)],
        ),
        out_shape=jax.ShapeDtypeStruct((count, rows, lags_out), jnp.bfloat16),
        cost_estimate=pl.CostEstimate(
            flops=count * rows * 2 * PERIOD * lags_out * 2 + count * offsets * 16 * capacity * group_bins,
            bytes_accessed=placed.size * 2 + white_sources.size * 2 + table.size * 2 + count * rows * lags_out * 2,
            transcendentals=0,
        ),
    )(ids, placed, white_sources, table)


def twiddle_table(lags_out):
    bin_index = np.arange(PERIOD, dtype=np.int64)
    lag_value = (np.arange(lags_out, dtype=np.int64) - lags_out // 2) * DEC
    phase = np.mod(bin_index[:, None] * lag_value[None, :], BINS).astype(np.float32)
    phase = (phase * np.float32(2.0 * math.pi / BINS)).astype(np.float64)
    table = np.concatenate([np.cos(phase), np.sin(phase)], axis=0)
    return table.astype(ml_dtypes.bfloat16)


def per_device(traces, sources, owner):
    blocks = lax.axis_size("blk")
    band_count = lax.axis_size("band")
    station_count = traces.shape[0]
    source_count = sources.shape[0]
    group_bins = traces.shape[2]
    capacity = max(2, 2 * station_count // blocks)
    lags_out = LAGS // DEC
    offsets = blocks // 4
    band = lax.axis_index("band")

    trace_float = traces.astype(jnp.float32)
    source_float = sources.astype(jnp.float32)
    trace_power, source_power = lax.psum(
        (
            jnp.sum(trace_float * trace_float, axis=(1, 2)),
            jnp.sum(source_float * source_float, axis=(1, 2)),
        ),
        "band",
    )
    white_sources = (
        source_float * lax.rsqrt(source_power / (2 * BINS) + EPS)[:, None, None]
    ).astype(jnp.bfloat16).reshape(1, source_count * 2, group_bins)
    white_traces = (
        (trace_float * lax.rsqrt(trace_power / (2 * BINS) + EPS)[:, None, None])
        .astype(jnp.bfloat16)
        .reshape(station_count, 2 * group_bins)
    )

    owners = owner[:, 0]
    owner_hits = (owners[:, None] == jnp.arange(blocks, dtype=jnp.int32)[None, :]).astype(jnp.int32)
    earlier = jnp.cumsum(owner_hits, axis=0) - owner_hits
    arrival = jnp.sum(owner_hits * earlier, axis=1)
    slot_index = owners * capacity + arrival
    placing = (
        jnp.arange(blocks * capacity, dtype=jnp.int32)[:, None] == slot_index[None, :]
    ).astype(jnp.bfloat16)
    placed = jnp.dot(placing, white_traces, preferred_element_type=jnp.float32).astype(jnp.bfloat16)
    placed = placed.reshape(blocks, capacity, 2, group_bins).transpose(0, 2, 1, 3)
    placed = placed.reshape(blocks, 2 * capacity, group_bins)

    table = jnp.asarray(twiddle_table(lags_out))

    me = lax.axis_index("blk")
    held = white_sources
    held_ids = me[None].astype(jnp.int32)
    bits = blocks.bit_length() - 1
    for bit in reversed(range(1, bits)):
        step = 1 << bit
        got = lax.ppermute(held, "blk", [(i, i ^ step) for i in range(blocks)])
        upper = jnp.bitwise_and(me // step, 1) == 1
        held = jnp.where(upper, jnp.concatenate([got, held]), jnp.concatenate([held, got]))
        got_ids = jnp.bitwise_xor(held_ids, step)
        held_ids = jnp.where(upper, jnp.concatenate([got_ids, held_ids]), jnp.concatenate([held_ids, got_ids]))
    got = lax.ppermute(held, "blk", [(i, i ^ 1) for i in range(blocks)])
    results = correlate(held_ids, placed, held, table, offsets, capacity)
    got_results = correlate(jnp.bitwise_xor(held_ids, 1), placed, got, table, offsets, capacity)
    upper = jnp.bitwise_and(me, 1) == 1
    results = jnp.where(
        upper, jnp.concatenate([got_results, results]), jnp.concatenate([results, got_results])
    )
    partial = results.reshape((2,) * bits + results.shape[1:])
    partial = partial.transpose(tuple(reversed(range(bits))) + tuple(range(bits, partial.ndim)))
    partial = partial.reshape(results.shape)
    arrived = lax.all_to_all(partial, "blk", split_axis=0, concat_axis=0, tiled=True)
    half = blocks // 2
    mine = lax.dynamic_slice_in_dim(arrived, band * half, half, axis=0)
    other = lax.dynamic_slice_in_dim(arrived, (1 - band) * half, half, axis=0)
    other = lax.ppermute(other, "band", [(0, 1), (1, 0)])
    summed = mine.astype(jnp.float32) + other.astype(jnp.float32)
    summed = summed.reshape(half, source_count, offsets, capacity, lags_out)
    return jnp.transpose(summed, (1, 2, 0, 3, 4)).reshape(
        source_count, offsets, half * capacity, lags_out
    )


def solution(mesh):
    placed = (P("blk", None, "band"), P("blk", None, "band"), P("blk", None))
    return jax.shard_map(
        per_device,
        mesh=mesh,
        in_specs=placed,
        out_specs=P("blk", None, "band", None),
        check_vma=False,
    )
```

```python
import functools
import math

import jax
import ml_dtypes
import numpy as np
import jax.numpy as jnp
from jax import lax
from jax.experimental import pallas as pl
from jax.experimental.pallas import tpu as pltpu
from jax.sharding import PartitionSpec as P

BINS = 8192
LAGS = 2048
DEC = 8
PERIOD = BINS // DEC


EPS = 1e-06


def correlate_kernel(blocks, offsets, capacity, group, norm_scale, placed_ref, source_ref, table_ref, out_ref, cross_ref):
    first = pl.program_id(0) * group
    folds = placed_ref.shape[2] // PERIOD
    rows = 2 * offsets * capacity
    for member in range(group):
        block = first + member
        for offset in range(offsets):
            owned = placed_ref[lax.rem(block - offset + blocks, blocks)].astype(jnp.float32)
            real_t = owned[:capacity]
            imag_t = owned[capacity:]
            for source in range(2):
                real_s = source_ref[member, 2 * source : 2 * source + 1].astype(jnp.float32)
                imag_s = source_ref[member, 2 * source + 1 : 2 * source + 2].astype(jnp.float32)
                even = real_t * real_s + imag_t * imag_s
                odd = real_t * imag_s - imag_t * real_s
                even_fold = even[:, :PERIOD]
                odd_fold = odd[:, :PERIOD]
                for fold in range(1, folds):
                    even_fold = even_fold + even[:, fold * PERIOD : (fold + 1) * PERIOD]
                    odd_fold = odd_fold + odd[:, fold * PERIOD : (fold + 1) * PERIOD]
                row = member * rows + (source * offsets + offset) * capacity
                cross_ref[row : row + capacity, :PERIOD] = even_fold
                cross_ref[row : row + capacity, PERIOD:] = odd_fold
    product = jnp.dot(
        cross_ref[...].astype(jnp.bfloat16), table_ref[...], preferred_element_type=jnp.float32
    )
    product = (product * norm_scale).astype(out_ref.dtype)
    for member in range(group):
        out_ref[member] = product[member * rows : (member + 1) * rows]


def correlate(placed, white_sources, table, offsets, capacity):
    blocks, _, group_bins = placed.shape
    rows = 2 * offsets * capacity
    lags_out = table.shape[1]
    group = 4
    body = functools.partial(correlate_kernel, blocks, offsets, capacity, group, BINS ** (-0.5))
    return pl.pallas_call(
        body,
        grid=(blocks // group,),
        in_specs=[
            pl.BlockSpec(placed.shape, lambda a: (0, 0, 0)),
            pl.BlockSpec((group,) + white_sources.shape[1:], lambda a: (a, 0, 0)),
            pl.BlockSpec(table.shape, lambda a: (0, 0)),
        ],
        out_specs=pl.BlockSpec((group, rows, lags_out), lambda a: (a, 0, 0)),
        out_shape=jax.ShapeDtypeStruct((blocks, rows, lags_out), jnp.bfloat16),
        scratch_shapes=[pltpu.VMEM((group * rows, 2 * PERIOD), jnp.float32)],
        cost_estimate=pl.CostEstimate(
            flops=blocks * rows * 2 * PERIOD * lags_out * 2 + blocks * offsets * 16 * capacity * group_bins,
            bytes_accessed=placed.size * 2 + white_sources.size * 2 + table.size * 2 + blocks * rows * lags_out * 2,
            transcendentals=0,
        ),
    )(placed, white_sources, table)


def twiddle_table(lags_out):
    bin_index = np.arange(PERIOD, dtype=np.int64)
    lag_value = (np.arange(lags_out, dtype=np.int64) - lags_out // 2) * DEC
    phase = np.mod(bin_index[:, None] * lag_value[None, :], BINS).astype(np.float32)
    phase = (phase * np.float32(2.0 * math.pi / BINS)).astype(np.float64)
    table = np.concatenate([np.cos(phase), np.sin(phase)], axis=0)
    return table.astype(ml_dtypes.bfloat16)


def per_device(traces, sources, owner):
    blocks = lax.axis_size("blk")
    band_count = lax.axis_size("band")
    station_count = traces.shape[0]
    source_count = sources.shape[0]
    group_bins = traces.shape[2]
    capacity = max(2, 2 * station_count // blocks)
    lags_out = LAGS // DEC
    offsets = blocks // 4
    band = lax.axis_index("band")

    trace_float = traces.astype(jnp.float32)
    source_float = sources.astype(jnp.float32)
    trace_power, source_power = lax.psum(
        (
            jnp.sum(trace_float * trace_float, axis=(1, 2)),
            jnp.sum(source_float * source_float, axis=(1, 2)),
        ),
        "band",
    )
    white_sources = (
        source_float * lax.rsqrt(source_power / (2 * BINS) + EPS)[:, None, None]
    ).astype(jnp.bfloat16)
    me = lax.axis_index("blk")
    held = white_sources[None]
    bits = blocks.bit_length() - 1
    shift = bits
    while shift > 0:
        width = 2 if shift >= 2 else 1
        shift -= width
        radix = 1 << width
        position = jnp.bitwise_and(me >> shift, radix - 1)
        widened = jnp.zeros((radix,) + held.shape, held.dtype)
        for partner in range(radix):
            if partner == 0:
                got = held
            else:
                route = [(i, i ^ (partner << shift)) for i in range(blocks)]
                got = lax.ppermute(held, "blk", route)
            widened = lax.dynamic_update_slice_in_dim(
                widened, got[None], jnp.bitwise_xor(position, partner), axis=0
            )
        held = widened
    groups = held.ndim - white_sources.ndim
    held = held.transpose(tuple(reversed(range(groups))) + tuple(range(groups, held.ndim)))
    white_traces = (
        (trace_float * lax.rsqrt(trace_power / (2 * BINS) + EPS)[:, None, None])
        .astype(jnp.bfloat16)
        .reshape(station_count, 2 * group_bins)
    )

    owners = owner[:, 0]
    owner_hits = (owners[:, None] == jnp.arange(blocks, dtype=jnp.int32)[None, :]).astype(jnp.int32)
    earlier = jnp.cumsum(owner_hits, axis=0) - owner_hits
    arrival = jnp.sum(owner_hits * earlier, axis=1)
    slot_index = owners * capacity + arrival
    placing = (
        jnp.arange(blocks * capacity, dtype=jnp.int32)[:, None] == slot_index[None, :]
    ).astype(jnp.bfloat16)
    placed = jnp.dot(placing, white_traces, preferred_element_type=jnp.float32).astype(jnp.bfloat16)
    placed = placed.reshape(blocks, capacity, 2, group_bins).transpose(0, 2, 1, 3)
    placed = placed.reshape(blocks, 2 * capacity, group_bins)

    table = jnp.asarray(twiddle_table(lags_out))

    white_sources = held.reshape(blocks, source_count * 2, group_bins)

    partial = correlate(placed, white_sources, table, offsets, capacity)
    arrived = lax.all_to_all(partial, "blk", split_axis=0, concat_axis=0, tiled=True)
    half = blocks // 2
    mine = lax.dynamic_slice_in_dim(arrived, band * half, half, axis=0)
    other = lax.dynamic_slice_in_dim(arrived, (1 - band) * half, half, axis=0)
    other = lax.ppermute(other, "band", [(0, 1), (1, 0)])
    summed = mine.astype(jnp.float32) + other.astype(jnp.float32)
    summed = summed.reshape(half, source_count, offsets, capacity, lags_out)
    return jnp.transpose(summed, (1, 2, 0, 3, 4)).reshape(
        source_count, offsets, half * capacity, lags_out
    )


def solution(mesh):
    placed = (P("blk", None, "band"), P("blk", None, "band"), P("blk", None))
    return jax.shard_map(
        per_device,
        mesh=mesh,
        in_specs=placed,
        out_specs=P("blk", None, "band", None),
        check_vma=False,
    )
```

```python
import functools
import math

import jax
import ml_dtypes
import numpy as np
import jax.numpy as jnp
from jax import lax
from jax.experimental import pallas as pl
from jax.experimental.pallas import tpu as pltpu
from jax.sharding import PartitionSpec as P

BINS = 8192
LAGS = 2048
DEC = 8
PERIOD = BINS // DEC


EPS = 1e-06


def correlate_kernel(blocks, offsets, capacity, group, norm_scale, placed_ref, source_ref, table_ref, out_ref, cross_ref):
    first = pl.program_id(0) * group
    folds = placed_ref.shape[2] // PERIOD
    rows = 2 * offsets * capacity
    for member in range(group):
        block = first + member
        for offset in range(offsets):
            owned = placed_ref[lax.rem(block - offset + blocks, blocks)]
            real_t = owned[:capacity]
            imag_t = owned[capacity:]
            for source in range(2):
                real_s = source_ref[member, 2 * source : 2 * source + 1]
                imag_s = source_ref[member, 2 * source + 1 : 2 * source + 2]
                even = real_t * real_s + imag_t * imag_s
                odd = real_t * imag_s - imag_t * real_s
                even_fold = even[:, :PERIOD]
                odd_fold = odd[:, :PERIOD]
                for fold in range(1, folds):
                    even_fold = even_fold + even[:, fold * PERIOD : (fold + 1) * PERIOD]
                    odd_fold = odd_fold + odd[:, fold * PERIOD : (fold + 1) * PERIOD]
                row = member * rows + (source * offsets + offset) * capacity
                cross_ref[row : row + capacity, :PERIOD] = even_fold.astype(jnp.float32)
                cross_ref[row : row + capacity, PERIOD:] = odd_fold.astype(jnp.float32)
    product = jnp.dot(
        cross_ref[...].astype(jnp.bfloat16), table_ref[...], preferred_element_type=jnp.float32
    )
    product = (product * norm_scale).astype(out_ref.dtype)
    for member in range(group):
        out_ref[member] = product[member * rows : (member + 1) * rows]


def correlate(placed, white_sources, table, offsets, capacity):
    blocks, _, group_bins = placed.shape
    rows = 2 * offsets * capacity
    lags_out = table.shape[1]
    group = 4
    body = functools.partial(correlate_kernel, blocks, offsets, capacity, group, BINS ** (-0.5))
    return pl.pallas_call(
        body,
        grid=(blocks // group,),
        in_specs=[
            pl.BlockSpec(placed.shape, lambda a: (0, 0, 0)),
            pl.BlockSpec((group,) + white_sources.shape[1:], lambda a: (a, 0, 0)),
            pl.BlockSpec(table.shape, lambda a: (0, 0)),
        ],
        out_specs=pl.BlockSpec((group, rows, lags_out), lambda a: (a, 0, 0)),
        out_shape=jax.ShapeDtypeStruct((blocks, rows, lags_out), jnp.bfloat16),
        scratch_shapes=[pltpu.VMEM((group * rows, 2 * PERIOD), jnp.float32)],
        cost_estimate=pl.CostEstimate(
            flops=blocks * rows * 2 * PERIOD * lags_out * 2 + blocks * offsets * 16 * capacity * group_bins,
            bytes_accessed=placed.size * 2 + white_sources.size * 2 + table.size * 2 + blocks * rows * lags_out * 2,
            transcendentals=0,
        ),
    )(placed, white_sources, table)


def twiddle_table(lags_out):
    bin_index = np.arange(PERIOD, dtype=np.int64)
    lag_value = (np.arange(lags_out, dtype=np.int64) - lags_out // 2) * DEC
    phase = np.mod(bin_index[:, None] * lag_value[None, :], BINS).astype(np.float32)
    phase = (phase * np.float32(2.0 * math.pi / BINS)).astype(np.float64)
    table = np.concatenate([np.cos(phase), np.sin(phase)], axis=0)
    return table.astype(ml_dtypes.bfloat16)


def per_device(traces, sources, owner):
    blocks = lax.axis_size("blk")
    band_count = lax.axis_size("band")
    station_count = traces.shape[0]
    source_count = sources.shape[0]
    group_bins = traces.shape[2]
    capacity = max(2, 2 * station_count // blocks)
    lags_out = LAGS // DEC
    offsets = blocks // 4
    band = lax.axis_index("band")

    trace_float = traces.astype(jnp.float32)
    source_float = sources.astype(jnp.float32)
    trace_power, source_power = lax.psum(
        (
            jnp.sum(trace_float * trace_float, axis=(1, 2)),
            jnp.sum(source_float * source_float, axis=(1, 2)),
        ),
        "band",
    )
    white_sources = (
        source_float * lax.rsqrt(source_power / (2 * BINS) + EPS)[:, None, None]
    ).astype(jnp.bfloat16)
    me = lax.axis_index("blk")
    held = white_sources[None]
    bits = blocks.bit_length() - 1
    shift = bits
    while shift > 0:
        width = 2 if shift >= 2 else 1
        shift -= width
        radix = 1 << width
        position = jnp.bitwise_and(me >> shift, radix - 1)
        widened = jnp.zeros((radix,) + held.shape, held.dtype)
        for partner in range(radix):
            if partner == 0:
                got = held
            else:
                route = [(i, i ^ (partner << shift)) for i in range(blocks)]
                got = lax.ppermute(held, "blk", route)
            widened = lax.dynamic_update_slice_in_dim(
                widened, got[None], jnp.bitwise_xor(position, partner), axis=0
            )
        held = widened
    groups = held.ndim - white_sources.ndim
    held = held.transpose(tuple(reversed(range(groups))) + tuple(range(groups, held.ndim)))
    white_traces = (
        (trace_float * lax.rsqrt(trace_power / (2 * BINS) + EPS)[:, None, None])
        .astype(jnp.bfloat16)
        .reshape(station_count, 2 * group_bins)
    )

    owners = owner[:, 0]
    owner_hits = (owners[:, None] == jnp.arange(blocks, dtype=jnp.int32)[None, :]).astype(jnp.int32)
    earlier = jnp.cumsum(owner_hits, axis=0) - owner_hits
    arrival = jnp.sum(owner_hits * earlier, axis=1)
    slot_index = owners * capacity + arrival
    placing = (
        jnp.arange(blocks * capacity, dtype=jnp.int32)[:, None] == slot_index[None, :]
    ).astype(jnp.bfloat16)
    placed = jnp.dot(placing, white_traces, preferred_element_type=jnp.float32).astype(jnp.bfloat16)
    placed = placed.reshape(blocks, capacity, 2, group_bins).transpose(0, 2, 1, 3)
    placed = placed.reshape(blocks, 2 * capacity, group_bins)

    table = jnp.asarray(twiddle_table(lags_out))

    white_sources = held.reshape(blocks, source_count * 2, group_bins)

    partial = correlate(placed, white_sources, table, offsets, capacity)
    arrived = lax.all_to_all(partial, "blk", split_axis=0, concat_axis=0, tiled=True)
    half = blocks // 2
    mine = lax.dynamic_slice_in_dim(arrived, band * half, half, axis=0)
    other = lax.dynamic_slice_in_dim(arrived, (1 - band) * half, half, axis=0)
    other = lax.ppermute(other, "band", [(0, 1), (1, 0)])
    summed = mine.astype(jnp.float32) + other.astype(jnp.float32)
    summed = summed.reshape(half, source_count, offsets, capacity, lags_out)
    return jnp.transpose(summed, (1, 2, 0, 3, 4)).reshape(
        source_count, offsets, half * capacity, lags_out
    )


def solution(mesh):
    placed = (P("blk", None, "band"), P("blk", None, "band"), P("blk", None))
    return jax.shard_map(
        per_device,
        mesh=mesh,
        in_specs=placed,
        out_specs=P("blk", None, "band", None),
        check_vma=False,
    )
```

```python
import functools
import math

import jax
import ml_dtypes
import numpy as np
import jax.numpy as jnp
from jax import lax
from jax.experimental import pallas as pl
from jax.experimental.pallas import tpu as pltpu
from jax.sharding import PartitionSpec as P

BINS = 8192
LAGS = 2048
DEC = 8
PERIOD = BINS // DEC


EPS = 1e-06


def correlate_kernel(blocks, offsets, capacity, group, norm_scale, placed_ref, source_ref, table_ref, out_ref, cross_ref):
    first = pl.program_id(0) * group
    folds = placed_ref.shape[2] // PERIOD
    rows = 2 * offsets * capacity
    for member in range(group):
        block = first + member
        for offset in range(offsets):
            owned = placed_ref[lax.rem(block - offset + blocks, blocks)]
            real_t = owned[:capacity]
            imag_t = owned[capacity:]
            for source in range(2):
                real_s = source_ref[member, 2 * source : 2 * source + 1]
                imag_s = source_ref[member, 2 * source + 1 : 2 * source + 2]
                even = real_t * real_s + imag_t * imag_s
                odd = real_t * imag_s - imag_t * real_s
                even_fold = even[:, :PERIOD]
                odd_fold = odd[:, :PERIOD]
                for fold in range(1, folds):
                    even_fold = even_fold + even[:, fold * PERIOD : (fold + 1) * PERIOD]
                    odd_fold = odd_fold + odd[:, fold * PERIOD : (fold + 1) * PERIOD]
                row = member * rows + (source * offsets + offset) * capacity
                cross_ref[row : row + capacity, :PERIOD] = even_fold.astype(jnp.float32)
                cross_ref[row : row + capacity, PERIOD:] = odd_fold.astype(jnp.float32)
    product = jnp.dot(
        cross_ref[...].astype(jnp.bfloat16), table_ref[...], preferred_element_type=jnp.float32
    )
    product = (product * norm_scale).astype(out_ref.dtype)
    for member in range(group):
        out_ref[member] = product[member * rows : (member + 1) * rows]


def correlate(placed, white_sources, table, offsets, capacity):
    blocks, _, group_bins = placed.shape
    rows = 2 * offsets * capacity
    lags_out = table.shape[1]
    group = 4
    body = functools.partial(correlate_kernel, blocks, offsets, capacity, group, BINS ** (-0.5))
    return pl.pallas_call(
        body,
        grid=(blocks // group,),
        in_specs=[
            pl.BlockSpec(placed.shape, lambda a: (0, 0, 0)),
            pl.BlockSpec((group,) + white_sources.shape[1:], lambda a: (a, 0, 0)),
            pl.BlockSpec(table.shape, lambda a: (0, 0)),
        ],
        out_specs=pl.BlockSpec((group, rows, lags_out), lambda a: (a, 0, 0)),
        out_shape=jax.ShapeDtypeStruct((blocks, rows, lags_out), jnp.bfloat16),
        scratch_shapes=[pltpu.VMEM((group * rows, 2 * PERIOD), jnp.float32)],
        cost_estimate=pl.CostEstimate(
            flops=blocks * rows * 2 * PERIOD * lags_out * 2 + blocks * offsets * 16 * capacity * group_bins,
            bytes_accessed=placed.size * 2 + white_sources.size * 2 + table.size * 2 + blocks * rows * lags_out * 2,
            transcendentals=0,
        ),
    )(placed, white_sources, table)


def twiddle_table(lags_out):
    bin_index = np.arange(PERIOD, dtype=np.int64)
    lag_value = (np.arange(lags_out, dtype=np.int64) - lags_out // 2) * DEC
    phase = np.mod(bin_index[:, None] * lag_value[None, :], BINS).astype(np.float32)
    phase = (phase * np.float32(2.0 * math.pi / BINS)).astype(np.float64)
    table = np.concatenate([np.cos(phase), np.sin(phase)], axis=0)
    return table.astype(ml_dtypes.bfloat16)


def per_device(traces, sources, owner):
    blocks = lax.axis_size("blk")
    band_count = lax.axis_size("band")
    station_count = traces.shape[0]
    source_count = sources.shape[0]
    group_bins = traces.shape[2]
    capacity = max(2, 2 * station_count // blocks)
    lags_out = LAGS // DEC
    offsets = blocks // 4
    band = lax.axis_index("band")

    trace_float = traces.astype(jnp.float32)
    source_float = sources.astype(jnp.float32)
    trace_power, source_power = lax.psum(
        (
            jnp.sum(trace_float * trace_float, axis=(1, 2)),
            jnp.sum(source_float * source_float, axis=(1, 2)),
        ),
        "band",
    )
    white_sources = (
        source_float * lax.rsqrt(source_power / (2 * BINS) + EPS)[:, None, None]
    ).astype(jnp.bfloat16)
    me = lax.axis_index("blk")
    held = white_sources[None]
    bits = blocks.bit_length() - 1
    shift = bits
    while shift > 0:
        width = 2 if shift >= 2 else 1
        shift -= width
        radix = 1 << width
        position = jnp.bitwise_and(me >> shift, radix - 1)
        widened = jnp.zeros((radix,) + held.shape, held.dtype)
        for partner in range(radix):
            if partner == 0:
                got = held
            else:
                route = [(i, i ^ (partner << shift)) for i in range(blocks)]
                got = lax.ppermute(held, "blk", route)
            widened = lax.dynamic_update_slice_in_dim(
                widened, got[None], jnp.bitwise_xor(position, partner), axis=0
            )
        held = widened
    groups = held.ndim - white_sources.ndim
    held = held.transpose(tuple(reversed(range(groups))) + tuple(range(groups, held.ndim)))
    owners = owner[:, 0]
    owner_hits = (owners[:, None] == jnp.arange(blocks, dtype=jnp.int32)[None, :]).astype(jnp.int32)
    earlier = jnp.cumsum(owner_hits, axis=0) - owner_hits
    arrival = jnp.sum(owner_hits * earlier, axis=1)
    slot_index = owners * capacity + arrival
    chosen = jnp.arange(blocks * capacity, dtype=jnp.int32)[:, None] == slot_index[None, :]
    raw_placed = jnp.dot(
        chosen.astype(jnp.bfloat16), traces.reshape(station_count, 2 * group_bins),
        preferred_element_type=jnp.float32,
    )
    station_scale = lax.rsqrt(trace_power / (2 * BINS) + EPS)
    slot_scale = jnp.sum(jnp.where(chosen, station_scale[None, :], 0.0), axis=1)
    placed = (raw_placed * slot_scale[:, None]).astype(jnp.bfloat16)
    placed = placed.reshape(blocks, capacity, 2, group_bins).transpose(0, 2, 1, 3)
    placed = placed.reshape(blocks, 2 * capacity, group_bins)

    table = jnp.asarray(twiddle_table(lags_out))

    white_sources = held.reshape(blocks, source_count * 2, group_bins)

    partial = correlate(placed, white_sources, table, offsets, capacity)
    arrived = lax.all_to_all(partial, "blk", split_axis=0, concat_axis=0, tiled=True)
    half = blocks // 2
    mine = lax.dynamic_slice_in_dim(arrived, band * half, half, axis=0)
    other = lax.dynamic_slice_in_dim(arrived, (1 - band) * half, half, axis=0)
    other = lax.ppermute(other, "band", [(0, 1), (1, 0)])
    summed = mine.astype(jnp.float32) + other.astype(jnp.float32)
    summed = summed.reshape(half, source_count, offsets, capacity, lags_out)
    return jnp.transpose(summed, (1, 2, 0, 3, 4)).reshape(
        source_count, offsets, half * capacity, lags_out
    )


def solution(mesh):
    placed = (P("blk", None, "band"), P("blk", None, "band"), P("blk", None))
    return jax.shard_map(
        per_device,
        mesh=mesh,
        in_specs=placed,
        out_specs=P("blk", None, "band", None),
        check_vma=False,
    )
```

```python
import functools
import math

import jax
import ml_dtypes
import numpy as np
import jax.numpy as jnp
from jax import lax
from jax.experimental import pallas as pl
from jax.experimental.pallas import tpu as pltpu
from jax.sharding import PartitionSpec as P

BINS = 8192
LAGS = 2048
DEC = 8
PERIOD = BINS // DEC


EPS = 1e-06


def correlate_kernel(blocks, offsets, capacity, group, norm_scale, placed_ref, source_ref, table_ref, out_ref, cross_ref):
    first = pl.program_id(0) * group
    folds = placed_ref.shape[2] // PERIOD
    rows = 2 * offsets * capacity
    for member in range(group):
        block = first + member
        for offset in range(offsets):
            owned = placed_ref[lax.rem(block - offset + blocks, blocks)]
            real_t = owned[:capacity]
            imag_t = owned[capacity:]
            for source in range(2):
                real_s = source_ref[member, 2 * source : 2 * source + 1]
                imag_s = source_ref[member, 2 * source + 1 : 2 * source + 2]
                even = real_t * real_s + imag_t * imag_s
                odd = real_t * imag_s - imag_t * real_s
                even_fold = even[:, :PERIOD]
                odd_fold = odd[:, :PERIOD]
                for fold in range(1, folds):
                    even_fold = even_fold + even[:, fold * PERIOD : (fold + 1) * PERIOD]
                    odd_fold = odd_fold + odd[:, fold * PERIOD : (fold + 1) * PERIOD]
                row = member * rows + (source * offsets + offset) * capacity
                cross_ref[row : row + capacity, :PERIOD] = even_fold.astype(jnp.float32)
                cross_ref[row : row + capacity, PERIOD:] = odd_fold.astype(jnp.float32)
    product = jnp.dot(
        cross_ref[...].astype(jnp.bfloat16), table_ref[...], preferred_element_type=jnp.float32
    )
    product = (product * norm_scale).astype(out_ref.dtype)
    for member in range(group):
        out_ref[member] = product[member * rows : (member + 1) * rows]


def correlate(placed, white_sources, table, offsets, capacity):
    blocks, _, group_bins = placed.shape
    rows = 2 * offsets * capacity
    lags_out = table.shape[1]
    group = 4
    body = functools.partial(correlate_kernel, blocks, offsets, capacity, group, BINS ** (-0.5))
    return pl.pallas_call(
        body,
        grid=(blocks // group,),
        in_specs=[
            pl.BlockSpec(placed.shape, lambda a: (0, 0, 0)),
            pl.BlockSpec((group,) + white_sources.shape[1:], lambda a: (a, 0, 0)),
            pl.BlockSpec(table.shape, lambda a: (0, 0)),
        ],
        out_specs=pl.BlockSpec((group, rows, lags_out), lambda a: (a, 0, 0)),
        out_shape=jax.ShapeDtypeStruct((blocks, rows, lags_out), jnp.bfloat16),
        scratch_shapes=[pltpu.VMEM((group * rows, 2 * PERIOD), jnp.float32)],
        cost_estimate=pl.CostEstimate(
            flops=blocks * rows * 2 * PERIOD * lags_out * 2 + blocks * offsets * 16 * capacity * group_bins,
            bytes_accessed=placed.size * 2 + white_sources.size * 2 + table.size * 2 + blocks * rows * lags_out * 2,
            transcendentals=0,
        ),
    )(placed, white_sources, table)


def twiddle_table(lags_out):
    bin_index = np.arange(PERIOD, dtype=np.int64)
    lag_value = (np.arange(lags_out, dtype=np.int64) - lags_out // 2) * DEC
    phase = np.mod(bin_index[:, None] * lag_value[None, :], BINS).astype(np.float32)
    phase = (phase * np.float32(2.0 * math.pi / BINS)).astype(np.float64)
    table = np.concatenate([np.cos(phase), np.sin(phase)], axis=0)
    return table.astype(ml_dtypes.bfloat16)


def per_device(traces, sources, owner):
    blocks = lax.axis_size("blk")
    band_count = lax.axis_size("band")
    station_count = traces.shape[0]
    source_count = sources.shape[0]
    group_bins = traces.shape[2]
    capacity = max(2, 2 * station_count // blocks)
    lags_out = LAGS // DEC
    offsets = blocks // 4
    band = lax.axis_index("band")

    source_float = sources.astype(jnp.float32)
    source_sums = jnp.sum(source_float * source_float, axis=(1, 2))
    source_power = source_sums + lax.ppermute(source_sums, "band", [(0, 1), (1, 0)])
    white_sources = (
        source_float * lax.rsqrt(source_power / (2 * BINS) + EPS)[:, None, None]
    ).astype(jnp.bfloat16)
    traces, white_sources = lax.optimization_barrier((traces, white_sources))
    trace_float = traces.astype(jnp.float32)
    trace_power = lax.psum(jnp.sum(trace_float * trace_float, axis=(1, 2)), "band")
    me = lax.axis_index("blk")
    held = white_sources[None]
    bits = blocks.bit_length() - 1
    shift = bits
    while shift > 0:
        width = 2 if shift >= 2 else 1
        shift -= width
        radix = 1 << width
        position = jnp.bitwise_and(me >> shift, radix - 1)
        widened = jnp.zeros((radix,) + held.shape, held.dtype)
        for partner in range(radix):
            if partner == 0:
                got = held
            else:
                route = [(i, i ^ (partner << shift)) for i in range(blocks)]
                got = lax.ppermute(held, "blk", route)
            widened = lax.dynamic_update_slice_in_dim(
                widened, got[None], jnp.bitwise_xor(position, partner), axis=0
            )
        held = widened
    groups = held.ndim - white_sources.ndim
    held = held.transpose(tuple(reversed(range(groups))) + tuple(range(groups, held.ndim)))
    owners = owner[:, 0]
    owner_hits = (owners[:, None] == jnp.arange(blocks, dtype=jnp.int32)[None, :]).astype(jnp.int32)
    earlier = jnp.cumsum(owner_hits, axis=0) - owner_hits
    arrival = jnp.sum(owner_hits * earlier, axis=1)
    slot_index = owners * capacity + arrival
    chosen = jnp.arange(blocks * capacity, dtype=jnp.int32)[:, None] == slot_index[None, :]
    raw_placed = jnp.dot(
        chosen.astype(jnp.bfloat16), traces.reshape(station_count, 2 * group_bins),
        preferred_element_type=jnp.float32,
    )
    station_scale = lax.rsqrt(trace_power / (2 * BINS) + EPS)
    slot_scale = jnp.sum(jnp.where(chosen, station_scale[None, :], 0.0), axis=1)
    placed = (raw_placed * slot_scale[:, None]).astype(jnp.bfloat16)
    placed = placed.reshape(blocks, capacity, 2, group_bins).transpose(0, 2, 1, 3)
    placed = placed.reshape(blocks, 2 * capacity, group_bins)

    table = jnp.asarray(twiddle_table(lags_out))

    white_sources = held.reshape(blocks, source_count * 2, group_bins)

    partial = correlate(placed, white_sources, table, offsets, capacity)
    arrived = lax.all_to_all(partial, "blk", split_axis=0, concat_axis=0, tiled=True)
    half = blocks // 2
    mine = lax.dynamic_slice_in_dim(arrived, band * half, half, axis=0)
    other = lax.dynamic_slice_in_dim(arrived, (1 - band) * half, half, axis=0)
    other = lax.ppermute(other, "band", [(0, 1), (1, 0)])
    summed = mine.astype(jnp.float32) + other.astype(jnp.float32)
    summed = summed.reshape(half, source_count, offsets, capacity, lags_out)
    return jnp.transpose(summed, (1, 2, 0, 3, 4)).reshape(
        source_count, offsets, half * capacity, lags_out
    )


def solution(mesh):
    placed = (P("blk", None, "band"), P("blk", None, "band"), P("blk", None))
    return jax.shard_map(
        per_device,
        mesh=mesh,
        in_specs=placed,
        out_specs=P("blk", None, "band", None),
        check_vma=False,
    )
```

```python
import functools
import math

import jax
import ml_dtypes
import numpy as np
import jax.numpy as jnp
from jax import lax
from jax.experimental import pallas as pl
from jax.experimental.pallas import tpu as pltpu
from jax.sharding import PartitionSpec as P

BINS = 8192
LAGS = 2048
DEC = 8
PERIOD = BINS // DEC


EPS = 1e-06


def correlate_kernel(blocks, offsets, capacity, group, norm_scale, placed_ref, source_ref, table_ref, out_ref, cross_ref):
    first = pl.program_id(0) * group
    folds = placed_ref.shape[2] // PERIOD
    rows = 2 * offsets * capacity
    for member in range(group):
        block = first + member
        for offset in range(offsets):
            owned = placed_ref[lax.rem(block - offset + blocks, blocks)]
            real_t = owned[:capacity]
            imag_t = owned[capacity:]
            for source in range(2):
                real_s = source_ref[member, 2 * source : 2 * source + 1]
                imag_s = source_ref[member, 2 * source + 1 : 2 * source + 2]
                even = real_t * real_s + imag_t * imag_s
                odd = real_t * imag_s - imag_t * real_s
                even_fold = even[:, :PERIOD]
                odd_fold = odd[:, :PERIOD]
                for fold in range(1, folds):
                    even_fold = even_fold + even[:, fold * PERIOD : (fold + 1) * PERIOD]
                    odd_fold = odd_fold + odd[:, fold * PERIOD : (fold + 1) * PERIOD]
                row = member * rows + (source * offsets + offset) * capacity
                cross_ref[row : row + capacity, :PERIOD] = even_fold.astype(jnp.float32)
                cross_ref[row : row + capacity, PERIOD:] = odd_fold.astype(jnp.float32)
    product = jnp.dot(
        cross_ref[...].astype(jnp.bfloat16), table_ref[...], preferred_element_type=jnp.float32
    )
    product = (product * norm_scale).astype(out_ref.dtype)
    for member in range(group):
        out_ref[member] = product[member * rows : (member + 1) * rows]


def correlate(placed, white_sources, table, offsets, capacity):
    blocks, _, group_bins = placed.shape
    rows = 2 * offsets * capacity
    lags_out = table.shape[1]
    group = 4
    body = functools.partial(correlate_kernel, blocks, offsets, capacity, group, BINS ** (-0.5))
    return pl.pallas_call(
        body,
        grid=(blocks // group,),
        in_specs=[
            pl.BlockSpec(placed.shape, lambda a: (0, 0, 0)),
            pl.BlockSpec((group,) + white_sources.shape[1:], lambda a: (a, 0, 0)),
            pl.BlockSpec(table.shape, lambda a: (0, 0)),
        ],
        out_specs=pl.BlockSpec((group, rows, lags_out), lambda a: (a, 0, 0)),
        out_shape=jax.ShapeDtypeStruct((blocks, rows, lags_out), jnp.bfloat16),
        scratch_shapes=[pltpu.VMEM((group * rows, 2 * PERIOD), jnp.float32)],
        cost_estimate=pl.CostEstimate(
            flops=blocks * rows * 2 * PERIOD * lags_out * 2 + blocks * offsets * 16 * capacity * group_bins,
            bytes_accessed=placed.size * 2 + white_sources.size * 2 + table.size * 2 + blocks * rows * lags_out * 2,
            transcendentals=0,
        ),
    )(placed, white_sources, table)


def twiddle_table(lags_out):
    bin_index = np.arange(PERIOD, dtype=np.int64)
    lag_value = (np.arange(lags_out, dtype=np.int64) - lags_out // 2) * DEC
    phase = np.mod(bin_index[:, None] * lag_value[None, :], BINS).astype(np.float32)
    phase = (phase * np.float32(2.0 * math.pi / BINS)).astype(np.float64)
    table = np.concatenate([np.cos(phase), np.sin(phase)], axis=0)
    return table.astype(ml_dtypes.bfloat16)


def per_device(traces, sources, owner):
    blocks = lax.axis_size("blk")
    band_count = lax.axis_size("band")
    station_count = traces.shape[0]
    source_count = sources.shape[0]
    group_bins = traces.shape[2]
    capacity = max(2, 2 * station_count // blocks)
    lags_out = LAGS // DEC
    offsets = blocks // 4
    band = lax.axis_index("band")

    trace_float = traces.astype(jnp.float32)
    source_float = sources.astype(jnp.float32)
    trace_power, source_power = lax.psum(
        (
            jnp.sum(trace_float * trace_float, axis=(1, 2)),
            jnp.sum(source_float * source_float, axis=(1, 2)),
        ),
        "band",
    )
    white_sources = (
        source_float * lax.rsqrt(source_power / (2 * BINS) + EPS)[:, None, None]
    ).astype(jnp.bfloat16)
    me = lax.axis_index("blk")
    held = white_sources[None]
    bits = blocks.bit_length() - 1
    shift = bits
    while shift > 0:
        width = 2 if shift >= 2 else 1
        shift -= width
        radix = 1 << width
        position = jnp.bitwise_and(me >> shift, radix - 1)
        widened = jnp.zeros((radix,) + held.shape, held.dtype)
        for partner in range(radix):
            if partner == 0:
                got = held
            else:
                route = [(i, i ^ (partner << shift)) for i in range(blocks)]
                got = lax.ppermute(held, "blk", route)
            widened = lax.dynamic_update_slice_in_dim(
                widened, got[None], jnp.bitwise_xor(position, partner), axis=0
            )
        held = widened
    groups = held.ndim - white_sources.ndim
    held = held.transpose(tuple(reversed(range(groups))) + tuple(range(groups, held.ndim)))
    owners = owner[:, 0]
    owner_hits = (owners[:, None] == jnp.arange(blocks, dtype=jnp.int32)[None, :]).astype(jnp.int32)
    earlier = jnp.cumsum(owner_hits, axis=0) - owner_hits
    arrival = jnp.sum(owner_hits * earlier, axis=1)
    slot_index = owners * capacity + arrival
    chosen = jnp.arange(blocks * capacity, dtype=jnp.int32)[:, None] == slot_index[None, :]
    raw_placed = jnp.dot(
        chosen.astype(jnp.bfloat16), traces.reshape(station_count, 2 * group_bins),
        preferred_element_type=jnp.float32,
    )
    station_scale = lax.rsqrt(trace_power / (2 * BINS) + EPS)
    slot_scale = jnp.sum(jnp.where(chosen, station_scale[None, :], 0.0), axis=1)
    placed = (raw_placed * slot_scale[:, None]).astype(jnp.bfloat16)
    placed = placed.reshape(blocks, capacity, 2, group_bins).transpose(0, 2, 1, 3)
    placed = placed.reshape(blocks, 2 * capacity, group_bins)

    table = jnp.asarray(twiddle_table(lags_out))

    white_sources = held.reshape(blocks, source_count * 2, group_bins)

    partial = correlate(placed, white_sources, table, offsets, capacity)
    rows = partial.shape[1] // source_count
    keep = lax.dynamic_slice_in_dim(partial, band * rows, rows, axis=1)
    give = lax.dynamic_slice_in_dim(partial, (1 - band) * rows, rows, axis=1)
    give = lax.ppermute(give, "band", [(0, 1), (1, 0)])
    summed = (keep.astype(jnp.float32) + give.astype(jnp.float32)).astype(jnp.bfloat16)
    arrived = lax.all_to_all(summed, "blk", split_axis=0, concat_axis=0, tiled=True)
    half = blocks // 2
    own_half = lax.dynamic_slice_in_dim(arrived, band * half, half, axis=0)
    other_half = lax.dynamic_slice_in_dim(arrived, (1 - band) * half, half, axis=0)
    other_source = lax.ppermute(other_half, "band", [(0, 1), (1, 0)])
    first = jnp.where(band == 0, own_half, other_source)
    second = jnp.where(band == 0, other_source, own_half)
    both = jnp.stack([first, second], axis=0).astype(jnp.float32)
    both = both.reshape(source_count, half, offsets, capacity, lags_out)
    return jnp.transpose(both, (0, 2, 1, 3, 4)).reshape(
        source_count, offsets, half * capacity, lags_out
    )


def solution(mesh):
    placed = (P("blk", None, "band"), P("blk", None, "band"), P("blk", None))
    return jax.shard_map(
        per_device,
        mesh=mesh,
        in_specs=placed,
        out_specs=P("blk", None, "band", None),
        check_vma=False,
    )
```

```python
import functools
import math

import jax
import ml_dtypes
import numpy as np
import jax.numpy as jnp
from jax import lax
from jax.experimental import pallas as pl
from jax.experimental.pallas import tpu as pltpu
from jax.sharding import PartitionSpec as P

BINS = 8192
LAGS = 2048
DEC = 8
PERIOD = BINS // DEC


EPS = 1e-06


def correlate_kernel(blocks, offsets, capacity, group, norm_scale, placed_ref, source_ref, table_ref, out_ref, cross_ref):
    first = pl.program_id(0) * group
    folds = placed_ref.shape[3] // PERIOD
    rows = 2 * offsets * capacity
    for member in range(group):
        block = first + member
        for offset in range(offsets):
            owner_block = lax.rem(block - offset + blocks, blocks)
            real_t = placed_ref[0, owner_block]
            imag_t = placed_ref[1, owner_block]
            for source in range(2):
                real_s = source_ref[member, 2 * source : 2 * source + 1]
                imag_s = source_ref[member, 2 * source + 1 : 2 * source + 2]
                even = real_t * real_s + imag_t * imag_s
                odd = real_t * imag_s - imag_t * real_s
                even_fold = even[:, :PERIOD]
                odd_fold = odd[:, :PERIOD]
                for fold in range(1, folds):
                    even_fold = even_fold + even[:, fold * PERIOD : (fold + 1) * PERIOD]
                    odd_fold = odd_fold + odd[:, fold * PERIOD : (fold + 1) * PERIOD]
                row = member * rows + (source * offsets + offset) * capacity
                cross_ref[row : row + capacity, :PERIOD] = even_fold.astype(jnp.float32)
                cross_ref[row : row + capacity, PERIOD:] = odd_fold.astype(jnp.float32)
    product = jnp.dot(
        cross_ref[...].astype(jnp.bfloat16), table_ref[...], preferred_element_type=jnp.float32
    )
    product = (product * norm_scale).astype(out_ref.dtype)
    for member in range(group):
        out_ref[member] = product[member * rows : (member + 1) * rows]


def correlate(placed, white_sources, table, offsets, capacity):
    _, blocks, _, group_bins = placed.shape
    rows = 2 * offsets * capacity
    lags_out = table.shape[1]
    group = 4
    body = functools.partial(correlate_kernel, blocks, offsets, capacity, group, BINS ** (-0.5))
    return pl.pallas_call(
        body,
        grid=(blocks // group,),
        in_specs=[
            pl.BlockSpec(placed.shape, lambda a: (0, 0, 0, 0)),
            pl.BlockSpec((group,) + white_sources.shape[1:], lambda a: (a, 0, 0)),
            pl.BlockSpec(table.shape, lambda a: (0, 0)),
        ],
        out_specs=pl.BlockSpec((group, rows, lags_out), lambda a: (a, 0, 0)),
        out_shape=jax.ShapeDtypeStruct((blocks, rows, lags_out), jnp.bfloat16),
        scratch_shapes=[pltpu.VMEM((group * rows, 2 * PERIOD), jnp.float32)],
        cost_estimate=pl.CostEstimate(
            flops=blocks * rows * 2 * PERIOD * lags_out * 2 + blocks * offsets * 16 * capacity * group_bins,
            bytes_accessed=placed.size * 2 + white_sources.size * 2 + table.size * 2 + blocks * rows * lags_out * 2,
            transcendentals=0,
        ),
    )(placed, white_sources, table)


def twiddle_table(lags_out):
    bin_index = np.arange(PERIOD, dtype=np.int64)
    lag_value = (np.arange(lags_out, dtype=np.int64) - lags_out // 2) * DEC
    phase = np.mod(bin_index[:, None] * lag_value[None, :], BINS).astype(np.float32)
    phase = (phase * np.float32(2.0 * math.pi / BINS)).astype(np.float64)
    table = np.concatenate([np.cos(phase), np.sin(phase)], axis=0)
    return table.astype(ml_dtypes.bfloat16)


def per_device(traces, sources, owner):
    blocks = lax.axis_size("blk")
    band_count = lax.axis_size("band")
    station_count = traces.shape[0]
    source_count = sources.shape[0]
    group_bins = traces.shape[2]
    capacity = max(2, 2 * station_count // blocks)
    lags_out = LAGS // DEC
    offsets = blocks // 4
    band = lax.axis_index("band")

    trace_float = traces.astype(jnp.float32)
    source_float = sources.astype(jnp.float32)
    trace_power, source_power = lax.psum(
        (
            jnp.sum(trace_float * trace_float, axis=(1, 2)),
            jnp.sum(source_float * source_float, axis=(1, 2)),
        ),
        "band",
    )
    white_sources = (
        source_float * lax.rsqrt(source_power / (2 * BINS) + EPS)[:, None, None]
    ).astype(jnp.bfloat16)
    me = lax.axis_index("blk")
    held = white_sources[None]
    bits = blocks.bit_length() - 1
    shift = bits
    while shift > 0:
        width = 2 if shift >= 2 else 1
        shift -= width
        radix = 1 << width
        position = jnp.bitwise_and(me >> shift, radix - 1)
        widened = jnp.zeros((radix,) + held.shape, held.dtype)
        for partner in range(radix):
            if partner == 0:
                got = held
            else:
                route = [(i, i ^ (partner << shift)) for i in range(blocks)]
                got = lax.ppermute(held, "blk", route)
            widened = lax.dynamic_update_slice_in_dim(
                widened, got[None], jnp.bitwise_xor(position, partner), axis=0
            )
        held = widened
    groups = held.ndim - white_sources.ndim
    held = held.transpose(tuple(reversed(range(groups))) + tuple(range(groups, held.ndim)))
    owners = owner[:, 0]
    owner_hits = (owners[:, None] == jnp.arange(blocks, dtype=jnp.int32)[None, :]).astype(jnp.int32)
    earlier = jnp.cumsum(owner_hits, axis=0) - owner_hits
    arrival = jnp.sum(owner_hits * earlier, axis=1)
    slot_index = owners * capacity + arrival
    chosen = jnp.arange(blocks * capacity, dtype=jnp.int32)[:, None] == slot_index[None, :]
    raw_placed = jnp.einsum(
        "si,ipk->psk", chosen.astype(jnp.bfloat16), traces, preferred_element_type=jnp.float32
    )
    station_scale = lax.rsqrt(trace_power / (2 * BINS) + EPS)
    slot_scale = jnp.sum(jnp.where(chosen, station_scale[None, :], 0.0), axis=1)
    placed = (raw_placed * slot_scale[None, :, None]).astype(jnp.bfloat16)
    placed = placed.reshape(2, blocks, capacity, group_bins)

    table = jnp.asarray(twiddle_table(lags_out))

    white_sources = held.reshape(blocks, source_count * 2, group_bins)

    partial = correlate(placed, white_sources, table, offsets, capacity)
    arrived = lax.all_to_all(partial, "blk", split_axis=0, concat_axis=0, tiled=True)
    half = blocks // 2
    mine = lax.dynamic_slice_in_dim(arrived, band * half, half, axis=0)
    other = lax.dynamic_slice_in_dim(arrived, (1 - band) * half, half, axis=0)
    other = lax.ppermute(other, "band", [(0, 1), (1, 0)])
    summed = mine.astype(jnp.float32) + other.astype(jnp.float32)
    summed = summed.reshape(half, source_count, offsets, capacity, lags_out)
    return jnp.transpose(summed, (1, 2, 0, 3, 4)).reshape(
        source_count, offsets, half * capacity, lags_out
    )


def solution(mesh):
    placed = (P("blk", None, "band"), P("blk", None, "band"), P("blk", None))
    return jax.shard_map(
        per_device,
        mesh=mesh,
        in_specs=placed,
        out_specs=P("blk", None, "band", None),
        check_vma=False,
    )
```

```python
import functools
import math

import jax
import ml_dtypes
import numpy as np
import jax.numpy as jnp
from jax import lax
from jax.experimental import pallas as pl
from jax.experimental.pallas import tpu as pltpu
from jax.sharding import PartitionSpec as P

BINS = 8192
LAGS = 2048
DEC = 8
PERIOD = BINS // DEC


EPS = 1e-06


def correlate_kernel(blocks, offsets, capacity, group, norm_scale, placed_ref, source_ref, table_ref, out_ref, cross_ref):
    first = pl.program_id(0) * group
    folds = placed_ref.shape[3] // PERIOD
    rows = 2 * offsets * capacity
    for member in range(group):
        block = first + member
        for offset in range(offsets):
            owner_block = lax.rem(block - offset + blocks, blocks)
            real_t = placed_ref[0, owner_block]
            imag_t = placed_ref[1, owner_block]
            for source in range(2):
                real_s = source_ref[member, 2 * source : 2 * source + 1]
                imag_s = source_ref[member, 2 * source + 1 : 2 * source + 2]
                even = real_t * real_s + imag_t * imag_s
                odd = real_t * imag_s - imag_t * real_s
                even_fold = even[:, :PERIOD]
                odd_fold = odd[:, :PERIOD]
                for fold in range(1, folds):
                    even_fold = even_fold + even[:, fold * PERIOD : (fold + 1) * PERIOD]
                    odd_fold = odd_fold + odd[:, fold * PERIOD : (fold + 1) * PERIOD]
                row = member * rows + (source * offsets + offset) * capacity
                cross_ref[row : row + capacity, :PERIOD] = even_fold.astype(jnp.float32)
                cross_ref[row : row + capacity, PERIOD:] = odd_fold.astype(jnp.float32)
    product = jnp.dot(
        cross_ref[...].astype(jnp.bfloat16), table_ref[...], preferred_element_type=jnp.float32
    )
    product = (product * norm_scale).astype(out_ref.dtype)
    for member in range(group):
        out_ref[member] = product[member * rows : (member + 1) * rows]


def correlate(placed, white_sources, table, offsets, capacity):
    _, blocks, _, group_bins = placed.shape
    rows = 2 * offsets * capacity
    lags_out = table.shape[1]
    group = 8
    body = functools.partial(correlate_kernel, blocks, offsets, capacity, group, BINS ** (-0.5))
    return pl.pallas_call(
        body,
        grid=(blocks // group,),
        in_specs=[
            pl.BlockSpec(placed.shape, lambda a: (0, 0, 0, 0)),
            pl.BlockSpec((group,) + white_sources.shape[1:], lambda a: (a, 0, 0)),
            pl.BlockSpec(table.shape, lambda a: (0, 0)),
        ],
        out_specs=pl.BlockSpec((group, rows, lags_out), lambda a: (a, 0, 0)),
        out_shape=jax.ShapeDtypeStruct((blocks, rows, lags_out), jnp.bfloat16),
        scratch_shapes=[pltpu.VMEM((group * rows, 2 * PERIOD), jnp.float32)],
        cost_estimate=pl.CostEstimate(
            flops=blocks * rows * 2 * PERIOD * lags_out * 2 + blocks * offsets * 16 * capacity * group_bins,
            bytes_accessed=placed.size * 2 + white_sources.size * 2 + table.size * 2 + blocks * rows * lags_out * 2,
            transcendentals=0,
        ),
    )(placed, white_sources, table)


def twiddle_table(lags_out):
    bin_index = np.arange(PERIOD, dtype=np.int64)
    lag_value = (np.arange(lags_out, dtype=np.int64) - lags_out // 2) * DEC
    phase = np.mod(bin_index[:, None] * lag_value[None, :], BINS).astype(np.float32)
    phase = (phase * np.float32(2.0 * math.pi / BINS)).astype(np.float64)
    table = np.concatenate([np.cos(phase), np.sin(phase)], axis=0)
    return table.astype(ml_dtypes.bfloat16)


def per_device(traces, sources, owner):
    blocks = lax.axis_size("blk")
    band_count = lax.axis_size("band")
    station_count = traces.shape[0]
    source_count = sources.shape[0]
    group_bins = traces.shape[2]
    capacity = max(2, 2 * station_count // blocks)
    lags_out = LAGS // DEC
    offsets = blocks // 4
    band = lax.axis_index("band")

    trace_float = traces.astype(jnp.float32)
    source_float = sources.astype(jnp.float32)
    trace_power, source_power = lax.psum(
        (
            jnp.sum(trace_float * trace_float, axis=(1, 2)),
            jnp.sum(source_float * source_float, axis=(1, 2)),
        ),
        "band",
    )
    white_sources = (
        source_float * lax.rsqrt(source_power / (2 * BINS) + EPS)[:, None, None]
    ).astype(jnp.bfloat16)
    me = lax.axis_index("blk")
    held = white_sources[None]
    bits = blocks.bit_length() - 1
    shift = bits
    while shift > 0:
        width = 2 if shift >= 2 else 1
        shift -= width
        radix = 1 << width
        position = jnp.bitwise_and(me >> shift, radix - 1)
        widened = jnp.zeros((radix,) + held.shape, held.dtype)
        for partner in range(radix):
            if partner == 0:
                got = held
            else:
                route = [(i, i ^ (partner << shift)) for i in range(blocks)]
                got = lax.ppermute(held, "blk", route)
            widened = lax.dynamic_update_slice_in_dim(
                widened, got[None], jnp.bitwise_xor(position, partner), axis=0
            )
        held = widened
    groups = held.ndim - white_sources.ndim
    held = held.transpose(tuple(reversed(range(groups))) + tuple(range(groups, held.ndim)))
    owners = owner[:, 0]
    owner_hits = (owners[:, None] == jnp.arange(blocks, dtype=jnp.int32)[None, :]).astype(jnp.int32)
    earlier = jnp.cumsum(owner_hits, axis=0) - owner_hits
    arrival = jnp.sum(owner_hits * earlier, axis=1)
    slot_index = owners * capacity + arrival
    chosen = jnp.arange(blocks * capacity, dtype=jnp.int32)[:, None] == slot_index[None, :]
    raw_placed = jnp.einsum(
        "si,ipk->psk", chosen.astype(jnp.bfloat16), traces, preferred_element_type=jnp.float32
    )
    station_scale = lax.rsqrt(trace_power / (2 * BINS) + EPS)
    slot_scale = jnp.sum(jnp.where(chosen, station_scale[None, :], 0.0), axis=1)
    placed = (raw_placed * slot_scale[None, :, None]).astype(jnp.bfloat16)
    placed = placed.reshape(2, blocks, capacity, group_bins)

    table = jnp.asarray(twiddle_table(lags_out))

    white_sources = held.reshape(blocks, source_count * 2, group_bins)

    partial = correlate(placed, white_sources, table, offsets, capacity)
    arrived = lax.all_to_all(partial, "blk", split_axis=0, concat_axis=0, tiled=True)
    half = blocks // 2
    mine = lax.dynamic_slice_in_dim(arrived, band * half, half, axis=0)
    other = lax.dynamic_slice_in_dim(arrived, (1 - band) * half, half, axis=0)
    other = lax.ppermute(other, "band", [(0, 1), (1, 0)])
    summed = mine.astype(jnp.float32) + other.astype(jnp.float32)
    summed = summed.reshape(half, source_count, offsets, capacity, lags_out)
    return jnp.transpose(summed, (1, 2, 0, 3, 4)).reshape(
        source_count, offsets, half * capacity, lags_out
    )


def solution(mesh):
    placed = (P("blk", None, "band"), P("blk", None, "band"), P("blk", None))
    return jax.shard_map(
        per_device,
        mesh=mesh,
        in_specs=placed,
        out_specs=P("blk", None, "band", None),
        check_vma=False,
    )
```

```python
import functools
import math

import jax
import ml_dtypes
import numpy as np
import jax.numpy as jnp
from jax import lax
from jax.experimental import pallas as pl
from jax.experimental.pallas import tpu as pltpu
from jax.sharding import PartitionSpec as P

BINS = 8192
LAGS = 2048
DEC = 8
PERIOD = BINS // DEC


EPS = 1e-06


def correlate_kernel(blocks, offsets, capacity, group, norm_scale, placed_ref, source_ref, table_ref, out_ref, cross_ref):
    first = pl.program_id(0) * group
    folds = placed_ref.shape[3] // PERIOD
    rows = 2 * offsets * capacity
    for member in range(group):
        block = first + member
        for offset in range(offsets):
            owner_block = lax.rem(block - offset + blocks, blocks)
            real_t = placed_ref[0, owner_block]
            imag_t = placed_ref[1, owner_block]
            for source in range(2):
                real_s = source_ref[member, 2 * source : 2 * source + 1]
                imag_s = source_ref[member, 2 * source + 1 : 2 * source + 2]
                even = real_t * real_s + imag_t * imag_s
                odd = real_t * imag_s - imag_t * real_s
                even_fold = even[:, :PERIOD]
                odd_fold = odd[:, :PERIOD]
                for fold in range(1, folds):
                    even_fold = even_fold + even[:, fold * PERIOD : (fold + 1) * PERIOD]
                    odd_fold = odd_fold + odd[:, fold * PERIOD : (fold + 1) * PERIOD]
                row = member * rows + (source * offsets + offset) * capacity
                cross_ref[row : row + capacity, :PERIOD] = even_fold.astype(jnp.float32)
                cross_ref[row : row + capacity, PERIOD:] = odd_fold.astype(jnp.float32)
    product = jnp.dot(
        cross_ref[...].astype(jnp.bfloat16), table_ref[...], preferred_element_type=jnp.float32
    )
    product = (product * norm_scale).astype(out_ref.dtype)
    for member in range(group):
        out_ref[member] = product[member * rows : (member + 1) * rows]


def correlate(placed, white_sources, table, offsets, capacity):
    _, blocks, _, group_bins = placed.shape
    rows = 2 * offsets * capacity
    lags_out = table.shape[1]
    group = 8
    body = functools.partial(correlate_kernel, blocks, offsets, capacity, group, BINS ** (-0.5))
    return pl.pallas_call(
        body,
        grid=(blocks // group,),
        in_specs=[
            pl.BlockSpec(placed.shape, lambda a: (0, 0, 0, 0)),
            pl.BlockSpec((group,) + white_sources.shape[1:], lambda a: (a, 0, 0)),
            pl.BlockSpec(table.shape, lambda a: (0, 0)),
        ],
        out_specs=pl.BlockSpec((group, rows, lags_out), lambda a: (a, 0, 0)),
        out_shape=jax.ShapeDtypeStruct((blocks, rows, lags_out), jnp.bfloat16),
        scratch_shapes=[pltpu.VMEM((group * rows, 2 * PERIOD), jnp.float32)],
        cost_estimate=pl.CostEstimate(
            flops=blocks * rows * 2 * PERIOD * lags_out * 2 + blocks * offsets * 16 * capacity * group_bins,
            bytes_accessed=placed.size * 2 + white_sources.size * 2 + table.size * 2 + blocks * rows * lags_out * 2,
            transcendentals=0,
        ),
    )(placed, white_sources, table)


def twiddle_table(lags_out):
    bin_index = np.arange(PERIOD, dtype=np.int64)
    lag_value = (np.arange(lags_out, dtype=np.int64) - lags_out // 2) * DEC
    phase = np.mod(bin_index[:, None] * lag_value[None, :], BINS).astype(np.float32)
    phase = (phase * np.float32(2.0 * math.pi / BINS)).astype(np.float64)
    table = np.concatenate([np.cos(phase), np.sin(phase)], axis=0)
    return table.astype(ml_dtypes.bfloat16)


def per_device(traces, sources, owner):
    blocks = lax.axis_size("blk")
    band_count = lax.axis_size("band")
    station_count = traces.shape[0]
    source_count = sources.shape[0]
    group_bins = traces.shape[2]
    capacity = max(2, 2 * station_count // blocks)
    lags_out = LAGS // DEC
    offsets = blocks // 4
    band = lax.axis_index("band")

    trace_float = traces.astype(jnp.float32)
    source_float = sources.astype(jnp.float32)
    trace_power, source_power = lax.psum(
        (
            jnp.sum(trace_float * trace_float, axis=(1, 2)),
            jnp.sum(source_float * source_float, axis=(1, 2)),
        ),
        "band",
    )
    white_sources = (
        source_float * lax.rsqrt(source_power / (2 * BINS) + EPS)[:, None, None]
    ).astype(jnp.bfloat16)
    me = lax.axis_index("blk")
    held = white_sources[None]
    bits = blocks.bit_length() - 1
    shift = bits
    while shift > 0:
        width = 2 if shift >= 2 else 1
        shift -= width
        radix = 1 << width
        position = jnp.bitwise_and(me >> shift, radix - 1)
        widened = jnp.zeros((radix,) + held.shape, held.dtype)
        for partner in range(radix):
            if partner == 0:
                got = held
            else:
                route = [(i, i ^ (partner << shift)) for i in range(blocks)]
                got = lax.ppermute(held, "blk", route)
            widened = lax.dynamic_update_slice_in_dim(
                widened, got[None], jnp.bitwise_xor(position, partner), axis=0
            )
        held = widened
    groups = held.ndim - white_sources.ndim
    held = held.transpose(tuple(reversed(range(groups))) + tuple(range(groups, held.ndim)))
    owners = owner[:, 0]
    owner_hits = (owners[:, None] == jnp.arange(blocks, dtype=jnp.int32)[None, :]).astype(jnp.int32)
    earlier = jnp.cumsum(owner_hits, axis=0) - owner_hits
    arrival = jnp.sum(owner_hits * earlier, axis=1)
    slot_index = owners * capacity + arrival
    chosen = jnp.arange(blocks * capacity, dtype=jnp.int32)[:, None] == slot_index[None, :]
    raw_placed = jnp.einsum(
        "si,ipk->psk", chosen.astype(jnp.bfloat16), traces, preferred_element_type=jnp.float32
    )
    station_scale = lax.rsqrt(trace_power / (2 * BINS) + EPS)
    slot_scale = jnp.sum(jnp.where(chosen, station_scale[None, :], 0.0), axis=1)
    placed = (raw_placed * slot_scale[None, :, None]).astype(jnp.bfloat16)
    placed = placed.reshape(2, blocks, capacity, group_bins)

    table = jnp.asarray(twiddle_table(lags_out))

    white_sources = held.reshape(blocks, source_count * 2, group_bins)

    partial = correlate(placed, white_sources, table, offsets, capacity)
    partial = partial.reshape(blocks, source_count, offsets, capacity, lags_out)
    arrived = lax.all_to_all(partial, "blk", split_axis=0, concat_axis=3, tiled=True)
    arrived = arrived.reshape(source_count, offsets, blocks * capacity, lags_out)
    half = blocks * capacity // 2
    mine = lax.dynamic_slice_in_dim(arrived, band * half, half, axis=2)
    other = lax.dynamic_slice_in_dim(arrived, (1 - band) * half, half, axis=2)
    other = lax.ppermute(other, "band", [(0, 1), (1, 0)])
    return mine.astype(jnp.float32) + other.astype(jnp.float32)


def solution(mesh):
    placed = (P("blk", None, "band"), P("blk", None, "band"), P("blk", None))
    return jax.shard_map(
        per_device,
        mesh=mesh,
        in_specs=placed,
        out_specs=P("blk", None, "band", None),
        check_vma=False,
    )
```

```python
import functools
import math

import jax
import ml_dtypes
import numpy as np
import jax.numpy as jnp
from jax import lax
from jax.experimental import pallas as pl
from jax.experimental.pallas import tpu as pltpu
from jax.sharding import PartitionSpec as P

BINS = 8192
LAGS = 2048
DEC = 8
PERIOD = BINS // DEC


EPS = 1e-06


def correlate_kernel(blocks, offsets, capacity, group, norm_scale, placed_ref, source_ref, table_ref, out_ref, cross_ref):
    first = pl.program_id(0) * group
    folds = placed_ref.shape[2] // PERIOD
    rows = 2 * offsets * capacity
    for member in range(group):
        block = first + member
        for offset in range(offsets):
            owned = placed_ref[lax.rem(block - offset + blocks, blocks)]
            real_t = owned[:capacity]
            imag_t = owned[capacity:]
            for source in range(2):
                real_s = source_ref[member, 2 * source : 2 * source + 1]
                imag_s = source_ref[member, 2 * source + 1 : 2 * source + 2]
                even = real_t * real_s + imag_t * imag_s
                odd = real_t * imag_s - imag_t * real_s
                even_fold = even[:, :PERIOD]
                odd_fold = odd[:, :PERIOD]
                for fold in range(1, folds):
                    even_fold = even_fold + even[:, fold * PERIOD : (fold + 1) * PERIOD]
                    odd_fold = odd_fold + odd[:, fold * PERIOD : (fold + 1) * PERIOD]
                row = member * rows + (source * offsets + offset) * capacity
                cross_ref[row : row + capacity, :PERIOD] = even_fold.astype(jnp.float32)
                cross_ref[row : row + capacity, PERIOD:] = odd_fold.astype(jnp.float32)
    product = jnp.dot(
        cross_ref[...].astype(jnp.bfloat16), table_ref[...], preferred_element_type=jnp.float32
    )
    product = (product * norm_scale).astype(out_ref.dtype)
    for member in range(group):
        out_ref[member] = product[member * rows : (member + 1) * rows]


def correlate(placed, white_sources, table, offsets, capacity):
    blocks, _, group_bins = placed.shape
    rows = 2 * offsets * capacity
    lags_out = table.shape[1]
    group = 8
    body = functools.partial(correlate_kernel, blocks, offsets, capacity, group, BINS ** (-0.5))
    return pl.pallas_call(
        body,
        grid=(blocks // group,),
        in_specs=[
            pl.BlockSpec(placed.shape, lambda a: (0, 0, 0)),
            pl.BlockSpec((group,) + white_sources.shape[1:], lambda a: (a, 0, 0)),
            pl.BlockSpec(table.shape, lambda a: (0, 0)),
        ],
        out_specs=pl.BlockSpec((group, rows, lags_out), lambda a: (a, 0, 0)),
        out_shape=jax.ShapeDtypeStruct((blocks, rows, lags_out), jnp.bfloat16),
        scratch_shapes=[pltpu.VMEM((group * rows, 2 * PERIOD), jnp.float32)],
        cost_estimate=pl.CostEstimate(
            flops=blocks * rows * 2 * PERIOD * lags_out * 2 + blocks * offsets * 16 * capacity * group_bins,
            bytes_accessed=placed.size * 2 + white_sources.size * 2 + table.size * 2 + blocks * rows * lags_out * 2,
            transcendentals=0,
        ),
    )(placed, white_sources, table)


def twiddle_table(lags_out):
    bin_index = np.arange(PERIOD, dtype=np.int64)
    lag_value = (np.arange(lags_out, dtype=np.int64) - lags_out // 2) * DEC
    phase = np.mod(bin_index[:, None] * lag_value[None, :], BINS).astype(np.float32)
    phase = (phase * np.float32(2.0 * math.pi / BINS)).astype(np.float64)
    table = np.concatenate([np.cos(phase), np.sin(phase)], axis=0)
    return table.astype(ml_dtypes.bfloat16)


def per_device(traces, sources, owner):
    blocks = lax.axis_size("blk")
    band_count = lax.axis_size("band")
    station_count = traces.shape[0]
    source_count = sources.shape[0]
    group_bins = traces.shape[2]
    capacity = max(2, 2 * station_count // blocks)
    lags_out = LAGS // DEC
    offsets = blocks // 4
    band = lax.axis_index("band")

    trace_float = traces.astype(jnp.float32)
    source_float = sources.astype(jnp.float32)
    trace_power, source_power = lax.psum(
        (
            jnp.sum(trace_float * trace_float, axis=(1, 2)),
            jnp.sum(source_float * source_float, axis=(1, 2)),
        ),
        "band",
    )
    white_sources = (
        source_float * lax.rsqrt(source_power / (2 * BINS) + EPS)[:, None, None]
    ).astype(jnp.bfloat16)
    me = lax.axis_index("blk")
    held = white_sources[None]
    bits = blocks.bit_length() - 1
    shift = bits
    while shift > 0:
        width = 2 if shift >= 2 else 1
        shift -= width
        radix = 1 << width
        position = jnp.bitwise_and(me >> shift, radix - 1)
        widened = jnp.zeros((radix,) + held.shape, held.dtype)
        for partner in range(radix):
            if partner == 0:
                got = held
            else:
                route = [(i, i ^ (partner << shift)) for i in range(blocks)]
                got = lax.ppermute(held, "blk", route)
            widened = lax.dynamic_update_slice_in_dim(
                widened, got[None], jnp.bitwise_xor(position, partner), axis=0
            )
        held = widened
    groups = held.ndim - white_sources.ndim
    held = held.transpose(tuple(reversed(range(groups))) + tuple(range(groups, held.ndim)))
    owners = owner[:, 0]
    owner_hits = (owners[:, None] == jnp.arange(blocks, dtype=jnp.int32)[None, :]).astype(jnp.int32)
    earlier = jnp.cumsum(owner_hits, axis=0) - owner_hits
    arrival = jnp.sum(owner_hits * earlier, axis=1)
    slot_index = owners * capacity + arrival
    chosen = jnp.arange(blocks * capacity, dtype=jnp.int32)[:, None] == slot_index[None, :]
    raw_placed = jnp.dot(
        chosen.astype(jnp.bfloat16), traces.reshape(station_count, 2 * group_bins),
        preferred_element_type=jnp.float32,
    )
    station_scale = lax.rsqrt(trace_power / (2 * BINS) + EPS)
    slot_scale = jnp.sum(jnp.where(chosen, station_scale[None, :], 0.0), axis=1)
    placed = (raw_placed * slot_scale[:, None]).astype(jnp.bfloat16)
    placed = placed.reshape(blocks, capacity, 2, group_bins).transpose(0, 2, 1, 3)
    placed = placed.reshape(blocks, 2 * capacity, group_bins)

    table = jnp.asarray(twiddle_table(lags_out))

    white_sources = held.reshape(blocks, source_count * 2, group_bins)

    partial = correlate(placed, white_sources, table, offsets, capacity)
    arrived = lax.all_to_all(partial, "blk", split_axis=0, concat_axis=0, tiled=True)
    half = blocks // 2
    mine = lax.dynamic_slice_in_dim(arrived, band * half, half, axis=0)
    other = lax.dynamic_slice_in_dim(arrived, (1 - band) * half, half, axis=0)
    other = lax.ppermute(other, "band", [(0, 1), (1, 0)])
    summed = mine.astype(jnp.float32) + other.astype(jnp.float32)
    summed = summed.reshape(half, source_count, offsets, capacity, lags_out)
    return jnp.transpose(summed, (1, 2, 0, 3, 4)).reshape(
        source_count, offsets, half * capacity, lags_out
    )


def solution(mesh):
    placed = (P("blk", None, "band"), P("blk", None, "band"), P("blk", None))
    return jax.shard_map(
        per_device,
        mesh=mesh,
        in_specs=placed,
        out_specs=P("blk", None, "band", None),
        check_vma=False,
    )
```

```python
import functools
import math

import jax
import ml_dtypes
import numpy as np
import jax.numpy as jnp
from jax import lax
from jax.experimental import pallas as pl
from jax.experimental.pallas import tpu as pltpu
from jax.sharding import PartitionSpec as P

BINS = 8192
LAGS = 2048
DEC = 8
PERIOD = BINS // DEC


EPS = 1e-06


def correlate_kernel(blocks, offsets, capacity, group, norm_scale, placed_ref, source_ref, table_ref, out_ref, cross_ref):
    first = pl.program_id(0) * group
    folds = placed_ref.shape[2] // PERIOD
    rows = 2 * offsets * capacity
    for member in range(group):
        block = first + member
        for offset in range(offsets):
            owned = placed_ref[lax.rem(block - offset + blocks, blocks)]
            real_t = owned[:capacity]
            imag_t = owned[capacity:]
            for source in range(2):
                real_s = source_ref[member, 2 * source : 2 * source + 1]
                imag_s = source_ref[member, 2 * source + 1 : 2 * source + 2]
                even = real_t * real_s + imag_t * imag_s
                odd = real_t * imag_s - imag_t * real_s
                even_fold = even[:, :PERIOD]
                odd_fold = odd[:, :PERIOD]
                for fold in range(1, folds):
                    even_fold = even_fold + even[:, fold * PERIOD : (fold + 1) * PERIOD]
                    odd_fold = odd_fold + odd[:, fold * PERIOD : (fold + 1) * PERIOD]
                row = member * rows + (source * offsets + offset) * capacity
                cross_ref[row : row + capacity, :PERIOD] = even_fold.astype(jnp.float32)
                cross_ref[row : row + capacity, PERIOD:] = odd_fold.astype(jnp.float32)
    product = jnp.dot(
        cross_ref[...].astype(jnp.bfloat16), table_ref[...], preferred_element_type=jnp.float32
    )
    product = (product * norm_scale).astype(out_ref.dtype)
    for member in range(group):
        out_ref[member] = product[member * rows : (member + 1) * rows]


def correlate(placed, white_sources, table, offsets, capacity):
    blocks, _, group_bins = placed.shape
    rows = 2 * offsets * capacity
    lags_out = table.shape[1]
    group = 16
    body = functools.partial(correlate_kernel, blocks, offsets, capacity, group, BINS ** (-0.5))
    return pl.pallas_call(
        body,
        grid=(blocks // group,),
        in_specs=[
            pl.BlockSpec(placed.shape, lambda a: (0, 0, 0)),
            pl.BlockSpec((group,) + white_sources.shape[1:], lambda a: (a, 0, 0)),
            pl.BlockSpec(table.shape, lambda a: (0, 0)),
        ],
        out_specs=pl.BlockSpec((group, rows, lags_out), lambda a: (a, 0, 0)),
        out_shape=jax.ShapeDtypeStruct((blocks, rows, lags_out), jnp.bfloat16),
        scratch_shapes=[pltpu.VMEM((group * rows, 2 * PERIOD), jnp.float32)],
        cost_estimate=pl.CostEstimate(
            flops=blocks * rows * 2 * PERIOD * lags_out * 2 + blocks * offsets * 16 * capacity * group_bins,
            bytes_accessed=placed.size * 2 + white_sources.size * 2 + table.size * 2 + blocks * rows * lags_out * 2,
            transcendentals=0,
        ),
    )(placed, white_sources, table)


def twiddle_table(lags_out):
    bin_index = np.arange(PERIOD, dtype=np.int64)
    lag_value = (np.arange(lags_out, dtype=np.int64) - lags_out // 2) * DEC
    phase = np.mod(bin_index[:, None] * lag_value[None, :], BINS).astype(np.float32)
    phase = (phase * np.float32(2.0 * math.pi / BINS)).astype(np.float64)
    table = np.concatenate([np.cos(phase), np.sin(phase)], axis=0)
    return table.astype(ml_dtypes.bfloat16)


def per_device(traces, sources, owner):
    blocks = lax.axis_size("blk")
    band_count = lax.axis_size("band")
    station_count = traces.shape[0]
    source_count = sources.shape[0]
    group_bins = traces.shape[2]
    capacity = max(2, 2 * station_count // blocks)
    lags_out = LAGS // DEC
    offsets = blocks // 4
    band = lax.axis_index("band")

    trace_float = traces.astype(jnp.float32)
    source_float = sources.astype(jnp.float32)
    trace_power, source_power = lax.psum(
        (
            jnp.sum(trace_float * trace_float, axis=(1, 2)),
            jnp.sum(source_float * source_float, axis=(1, 2)),
        ),
        "band",
    )
    white_sources = (
        source_float * lax.rsqrt(source_power / (2 * BINS) + EPS)[:, None, None]
    ).astype(jnp.bfloat16)
    me = lax.axis_index("blk")
    held = white_sources[None]
    bits = blocks.bit_length() - 1
    shift = bits
    while shift > 0:
        width = 2 if shift >= 2 else 1
        shift -= width
        radix = 1 << width
        position = jnp.bitwise_and(me >> shift, radix - 1)
        widened = jnp.zeros((radix,) + held.shape, held.dtype)
        for partner in range(radix):
            if partner == 0:
                got = held
            else:
                route = [(i, i ^ (partner << shift)) for i in range(blocks)]
                got = lax.ppermute(held, "blk", route)
            widened = lax.dynamic_update_slice_in_dim(
                widened, got[None], jnp.bitwise_xor(position, partner), axis=0
            )
        held = widened
    groups = held.ndim - white_sources.ndim
    held = held.transpose(tuple(reversed(range(groups))) + tuple(range(groups, held.ndim)))
    owners = owner[:, 0]
    owner_hits = (owners[:, None] == jnp.arange(blocks, dtype=jnp.int32)[None, :]).astype(jnp.int32)
    earlier = jnp.cumsum(owner_hits, axis=0) - owner_hits
    arrival = jnp.sum(owner_hits * earlier, axis=1)
    slot_index = owners * capacity + arrival
    chosen = jnp.arange(blocks * capacity, dtype=jnp.int32)[:, None] == slot_index[None, :]
    raw_placed = jnp.dot(
        chosen.astype(jnp.bfloat16), traces.reshape(station_count, 2 * group_bins),
        preferred_element_type=jnp.float32,
    )
    station_scale = lax.rsqrt(trace_power / (2 * BINS) + EPS)
    slot_scale = jnp.sum(jnp.where(chosen, station_scale[None, :], 0.0), axis=1)
    placed = (raw_placed * slot_scale[:, None]).astype(jnp.bfloat16)
    placed = placed.reshape(blocks, capacity, 2, group_bins).transpose(0, 2, 1, 3)
    placed = placed.reshape(blocks, 2 * capacity, group_bins)

    table = jnp.asarray(twiddle_table(lags_out))

    white_sources = held.reshape(blocks, source_count * 2, group_bins)

    partial = correlate(placed, white_sources, table, offsets, capacity)
    arrived = lax.all_to_all(partial, "blk", split_axis=0, concat_axis=0, tiled=True)
    half = blocks // 2
    mine = lax.dynamic_slice_in_dim(arrived, band * half, half, axis=0)
    other = lax.dynamic_slice_in_dim(arrived, (1 - band) * half, half, axis=0)
    other = lax.ppermute(other, "band", [(0, 1), (1, 0)])
    summed = mine.astype(jnp.float32) + other.astype(jnp.float32)
    summed = summed.reshape(half, source_count, offsets, capacity, lags_out)
    return jnp.transpose(summed, (1, 2, 0, 3, 4)).reshape(
        source_count, offsets, half * capacity, lags_out
    )


def solution(mesh):
    placed = (P("blk", None, "band"), P("blk", None, "band"), P("blk", None))
    return jax.shard_map(
        per_device,
        mesh=mesh,
        in_specs=placed,
        out_specs=P("blk", None, "band", None),
        check_vma=False,
    )
```

```python
import functools
import math

import jax
import ml_dtypes
import numpy as np
import jax.numpy as jnp
from jax import lax
from jax.experimental import pallas as pl
from jax.experimental.pallas import tpu as pltpu
from jax.sharding import PartitionSpec as P

BINS = 8192
LAGS = 2048
DEC = 8
PERIOD = BINS // DEC


EPS = 1e-06


def correlate_kernel(blocks, offsets, capacity, group, norm_scale, placed_ref, source_ref, table_ref, out_ref, cross_ref):
    first = pl.program_id(0) * group
    folds = placed_ref.shape[2] // PERIOD
    rows = 2 * offsets * capacity
    for member in range(group):
        block = first + member
        for offset in range(offsets):
            owned = placed_ref[lax.rem(block - offset + blocks, blocks)]
            real_t = owned[:capacity]
            imag_t = owned[capacity:]
            for source in range(2):
                real_s = source_ref[member, 2 * source : 2 * source + 1]
                imag_s = source_ref[member, 2 * source + 1 : 2 * source + 2]
                even = real_t * real_s + imag_t * imag_s
                odd = real_t * imag_s - imag_t * real_s
                even_fold = even[:, :PERIOD]
                odd_fold = odd[:, :PERIOD]
                for fold in range(1, folds):
                    even_fold = even_fold + even[:, fold * PERIOD : (fold + 1) * PERIOD]
                    odd_fold = odd_fold + odd[:, fold * PERIOD : (fold + 1) * PERIOD]
                row = member * rows + (source * offsets + offset) * capacity
                cross_ref[row : row + capacity, :PERIOD] = even_fold.astype(jnp.float32)
                cross_ref[row : row + capacity, PERIOD:] = odd_fold.astype(jnp.float32)
    product = jnp.dot(
        cross_ref[...].astype(jnp.bfloat16), table_ref[...], preferred_element_type=jnp.float32
    )
    product = (product * norm_scale).astype(out_ref.dtype)
    for member in range(group):
        out_ref[member] = product[member * rows : (member + 1) * rows]


def correlate(placed, white_sources, table, offsets, capacity):
    blocks, _, group_bins = placed.shape
    rows = 2 * offsets * capacity
    lags_out = table.shape[1]
    group = 8
    body = functools.partial(correlate_kernel, blocks, offsets, capacity, group, BINS ** (-0.5))
    return pl.pallas_call(
        body,
        grid=(blocks // group,),
        in_specs=[
            pl.BlockSpec(placed.shape, lambda a: (0, 0, 0)),
            pl.BlockSpec((group,) + white_sources.shape[1:], lambda a: (a, 0, 0)),
            pl.BlockSpec(table.shape, lambda a: (0, 0)),
        ],
        out_specs=pl.BlockSpec((group, rows, lags_out), lambda a: (a, 0, 0)),
        out_shape=jax.ShapeDtypeStruct((blocks, rows, lags_out), jnp.bfloat16),
        scratch_shapes=[pltpu.VMEM((group * rows, 2 * PERIOD), jnp.float32)],
        cost_estimate=pl.CostEstimate(
            flops=blocks * rows * 2 * PERIOD * lags_out * 2 + blocks * offsets * 16 * capacity * group_bins,
            bytes_accessed=placed.size * 2 + white_sources.size * 2 + table.size * 2 + blocks * rows * lags_out * 2,
            transcendentals=0,
        ),
    )(placed, white_sources, table)


def twiddle_table(lags_out):
    bin_index = np.arange(PERIOD, dtype=np.int64)
    lag_value = (np.arange(lags_out, dtype=np.int64) - lags_out // 2) * DEC
    phase = np.mod(bin_index[:, None] * lag_value[None, :], BINS).astype(np.float32)
    phase = (phase * np.float32(2.0 * math.pi / BINS)).astype(np.float64)
    table = np.concatenate([np.cos(phase), np.sin(phase)], axis=0)
    return table.astype(ml_dtypes.bfloat16)


def per_device(traces, sources, owner):
    blocks = lax.axis_size("blk")
    band_count = lax.axis_size("band")
    station_count = traces.shape[0]
    source_count = sources.shape[0]
    group_bins = traces.shape[2]
    capacity = max(2, 2 * station_count // blocks)
    lags_out = LAGS // DEC
    offsets = blocks // 4
    band = lax.axis_index("band")

    trace_float = traces.astype(jnp.float32)
    source_float = sources.astype(jnp.float32)
    lane_sums = jnp.sum(
        (trace_float * trace_float).reshape(station_count, 2, group_bins // 128, 128), axis=(1, 2)
    )
    lane_sums = lax.optimization_barrier(lane_sums)
    trace_power, source_power = lax.psum(
        (
            jnp.sum(lane_sums, axis=1),
            jnp.sum(source_float * source_float, axis=(1, 2)),
        ),
        "band",
    )
    white_sources = (
        source_float * lax.rsqrt(source_power / (2 * BINS) + EPS)[:, None, None]
    ).astype(jnp.bfloat16)
    me = lax.axis_index("blk")
    held = white_sources[None]
    bits = blocks.bit_length() - 1
    shift = bits
    while shift > 0:
        width = 2 if shift >= 2 else 1
        shift -= width
        radix = 1 << width
        position = jnp.bitwise_and(me >> shift, radix - 1)
        widened = jnp.zeros((radix,) + held.shape, held.dtype)
        for partner in range(radix):
            if partner == 0:
                got = held
            else:
                route = [(i, i ^ (partner << shift)) for i in range(blocks)]
                got = lax.ppermute(held, "blk", route)
            widened = lax.dynamic_update_slice_in_dim(
                widened, got[None], jnp.bitwise_xor(position, partner), axis=0
            )
        held = widened
    groups = held.ndim - white_sources.ndim
    held = held.transpose(tuple(reversed(range(groups))) + tuple(range(groups, held.ndim)))
    owners = owner[:, 0]
    owner_hits = (owners[:, None] == jnp.arange(blocks, dtype=jnp.int32)[None, :]).astype(jnp.int32)
    earlier = jnp.cumsum(owner_hits, axis=0) - owner_hits
    arrival = jnp.sum(owner_hits * earlier, axis=1)
    slot_index = owners * capacity + arrival
    chosen = jnp.arange(blocks * capacity, dtype=jnp.int32)[:, None] == slot_index[None, :]
    raw_placed = jnp.dot(
        chosen.astype(jnp.bfloat16), traces.reshape(station_count, 2 * group_bins),
        preferred_element_type=jnp.float32,
    )
    station_scale = lax.rsqrt(trace_power / (2 * BINS) + EPS)
    slot_scale = jnp.sum(jnp.where(chosen, station_scale[None, :], 0.0), axis=1)
    placed = (raw_placed * slot_scale[:, None]).astype(jnp.bfloat16)
    placed = placed.reshape(blocks, capacity, 2, group_bins).transpose(0, 2, 1, 3)
    placed = placed.reshape(blocks, 2 * capacity, group_bins)

    table = jnp.asarray(twiddle_table(lags_out))

    white_sources = held.reshape(blocks, source_count * 2, group_bins)

    partial = correlate(placed, white_sources, table, offsets, capacity)
    arrived = lax.all_to_all(partial, "blk", split_axis=0, concat_axis=0, tiled=True)
    half = blocks // 2
    mine = lax.dynamic_slice_in_dim(arrived, band * half, half, axis=0)
    other = lax.dynamic_slice_in_dim(arrived, (1 - band) * half, half, axis=0)
    other = lax.ppermute(other, "band", [(0, 1), (1, 0)])
    summed = mine.astype(jnp.float32) + other.astype(jnp.float32)
    summed = summed.reshape(half, source_count, offsets, capacity, lags_out)
    return jnp.transpose(summed, (1, 2, 0, 3, 4)).reshape(
        source_count, offsets, half * capacity, lags_out
    )


def solution(mesh):
    placed = (P("blk", None, "band"), P("blk", None, "band"), P("blk", None))
    return jax.shard_map(
        per_device,
        mesh=mesh,
        in_specs=placed,
        out_specs=P("blk", None, "band", None),
        check_vma=False,
    )
```

```python
import functools
import math

import jax
import ml_dtypes
import numpy as np
import jax.numpy as jnp
from jax import lax
from jax.experimental import pallas as pl
from jax.experimental.pallas import tpu as pltpu
from jax.sharding import PartitionSpec as P

BINS = 8192
LAGS = 2048
DEC = 8
PERIOD = BINS // DEC


EPS = 1e-06


def correlate_kernel(blocks, offsets, capacity, group, norm_scale, placed_ref, source_ref, table_ref, out_ref, cross_ref):
    first = pl.program_id(0) * group
    folds = placed_ref.shape[2] // PERIOD
    rows = 2 * offsets * capacity
    for member in range(group):
        block = first + member
        for offset in range(offsets):
            owned = placed_ref[lax.rem(block - offset + blocks, blocks)]
            real_t = owned[:capacity]
            imag_t = owned[capacity:]
            for source in range(2):
                real_s = source_ref[member, source, 0:1]
                imag_s = source_ref[member, source, 1:2]
                even = real_t * real_s + imag_t * imag_s
                odd = real_t * imag_s - imag_t * real_s
                even_fold = even[:, :PERIOD]
                odd_fold = odd[:, :PERIOD]
                for fold in range(1, folds):
                    even_fold = even_fold + even[:, fold * PERIOD : (fold + 1) * PERIOD]
                    odd_fold = odd_fold + odd[:, fold * PERIOD : (fold + 1) * PERIOD]
                row = member * rows + (source * offsets + offset) * capacity
                cross_ref[row : row + capacity, :PERIOD] = even_fold.astype(jnp.float32)
                cross_ref[row : row + capacity, PERIOD:] = odd_fold.astype(jnp.float32)
    product = jnp.dot(
        cross_ref[...].astype(jnp.bfloat16), table_ref[...], preferred_element_type=jnp.float32
    )
    product = (product * norm_scale).astype(out_ref.dtype)
    for member in range(group):
        out_ref[member] = product[member * rows : (member + 1) * rows]


def correlate(placed, white_sources, table, offsets, capacity):
    blocks, _, group_bins = placed.shape
    rows = 2 * offsets * capacity
    lags_out = table.shape[1]
    group = 8
    body = functools.partial(correlate_kernel, blocks, offsets, capacity, group, BINS ** (-0.5))
    return pl.pallas_call(
        body,
        grid=(blocks // group,),
        in_specs=[
            pl.BlockSpec(placed.shape, lambda a: (0, 0, 0)),
            pl.BlockSpec((group,) + white_sources.shape[1:], lambda a: (a, 0, 0, 0)),
            pl.BlockSpec(table.shape, lambda a: (0, 0)),
        ],
        out_specs=pl.BlockSpec((group, rows, lags_out), lambda a: (a, 0, 0)),
        out_shape=jax.ShapeDtypeStruct((blocks, rows, lags_out), jnp.bfloat16),
        scratch_shapes=[pltpu.VMEM((group * rows, 2 * PERIOD), jnp.float32)],
        cost_estimate=pl.CostEstimate(
            flops=blocks * rows * 2 * PERIOD * lags_out * 2 + blocks * offsets * 16 * capacity * group_bins,
            bytes_accessed=placed.size * 2 + white_sources.size * 2 + table.size * 2 + blocks * rows * lags_out * 2,
            transcendentals=0,
        ),
    )(placed, white_sources, table)


def twiddle_table(lags_out):
    bin_index = np.arange(PERIOD, dtype=np.int64)
    lag_value = (np.arange(lags_out, dtype=np.int64) - lags_out // 2) * DEC
    phase = np.mod(bin_index[:, None] * lag_value[None, :], BINS).astype(np.float32)
    phase = (phase * np.float32(2.0 * math.pi / BINS)).astype(np.float64)
    table = np.concatenate([np.cos(phase), np.sin(phase)], axis=0)
    return table.astype(ml_dtypes.bfloat16)


def per_device(traces, sources, owner):
    blocks = lax.axis_size("blk")
    band_count = lax.axis_size("band")
    station_count = traces.shape[0]
    source_count = sources.shape[0]
    group_bins = traces.shape[2]
    capacity = max(2, 2 * station_count // blocks)
    lags_out = LAGS // DEC
    offsets = blocks // 4
    band = lax.axis_index("band")

    trace_float = traces.astype(jnp.float32)
    source_float = sources.astype(jnp.float32)
    trace_power, source_power = lax.psum(
        (
            jnp.sum(trace_float * trace_float, axis=(1, 2)),
            jnp.sum(source_float * source_float, axis=(1, 2)),
        ),
        "band",
    )
    white_sources = (
        source_float * lax.rsqrt(source_power / (2 * BINS) + EPS)[:, None, None]
    ).astype(jnp.bfloat16)
    me = lax.axis_index("blk")
    held = white_sources[None]
    bits = blocks.bit_length() - 1
    shift = bits
    grouped = 1
    while shift > 0:
        width = 2 if shift >= 2 else 1
        shift -= width
        radix = 1 << width
        position = jnp.bitwise_and(me >> shift, radix - 1)
        widened = jnp.zeros(held.shape[:grouped] + (radix,) + held.shape[grouped:], held.dtype)
        rest = (0,) * (held.ndim - grouped)
        for partner in range(radix):
            if partner == 0:
                got = held
            else:
                route = [(i, i ^ (partner << shift)) for i in range(blocks)]
                got = lax.ppermute(held, "blk", route)
            start = (0,) * grouped + (jnp.bitwise_xor(position, partner),) + rest
            widened = lax.dynamic_update_slice(widened, jnp.expand_dims(got, grouped), start)
        held = widened
        grouped += 1
    held = held.reshape((blocks,) + white_sources.shape)
    owners = owner[:, 0]
    owner_hits = (owners[:, None] == jnp.arange(blocks, dtype=jnp.int32)[None, :]).astype(jnp.int32)
    earlier = jnp.cumsum(owner_hits, axis=0) - owner_hits
    arrival = jnp.sum(owner_hits * earlier, axis=1)
    slot_index = owners * capacity + arrival
    chosen = jnp.arange(blocks * capacity, dtype=jnp.int32)[:, None] == slot_index[None, :]
    raw_placed = jnp.dot(
        chosen.astype(jnp.bfloat16), traces.reshape(station_count, 2 * group_bins),
        preferred_element_type=jnp.float32,
    )
    station_scale = lax.rsqrt(trace_power / (2 * BINS) + EPS)
    slot_scale = jnp.sum(jnp.where(chosen, station_scale[None, :], 0.0), axis=1)
    placed = (raw_placed * slot_scale[:, None]).astype(jnp.bfloat16)
    placed = placed.reshape(blocks, capacity, 2, group_bins).transpose(0, 2, 1, 3)
    placed = placed.reshape(blocks, 2 * capacity, group_bins)

    table = jnp.asarray(twiddle_table(lags_out))

    white_sources = held

    partial = correlate(placed, white_sources, table, offsets, capacity)
    arrived = lax.all_to_all(partial, "blk", split_axis=0, concat_axis=0, tiled=True)
    half = blocks // 2
    mine = lax.dynamic_slice_in_dim(arrived, band * half, half, axis=0)
    other = lax.dynamic_slice_in_dim(arrived, (1 - band) * half, half, axis=0)
    other = lax.ppermute(other, "band", [(0, 1), (1, 0)])
    summed = mine.astype(jnp.float32) + other.astype(jnp.float32)
    summed = summed.reshape(half, source_count, offsets, capacity, lags_out)
    return jnp.transpose(summed, (1, 2, 0, 3, 4)).reshape(
        source_count, offsets, half * capacity, lags_out
    )


def solution(mesh):
    placed = (P("blk", None, "band"), P("blk", None, "band"), P("blk", None))
    return jax.shard_map(
        per_device,
        mesh=mesh,
        in_specs=placed,
        out_specs=P("blk", None, "band", None),
        check_vma=False,
    )
```

```python
import functools
import math

import jax
import ml_dtypes
import numpy as np
import jax.numpy as jnp
from jax import lax
from jax.experimental import pallas as pl
from jax.experimental.pallas import tpu as pltpu
from jax.sharding import PartitionSpec as P

BINS = 8192
LAGS = 2048
DEC = 8
PERIOD = BINS // DEC


EPS = 1e-06


def correlate_kernel(blocks, offsets, capacity, group, norm_scale, placed_ref, source_ref, table_ref, out_ref, cross_ref):
    first = pl.program_id(0) * group
    folds = placed_ref.shape[2] // PERIOD
    rows = 2 * offsets * capacity
    for member in range(group):
        block = first + member
        for offset in range(offsets):
            owned = placed_ref[lax.rem(block - offset + blocks, blocks)]
            real_t = owned[:capacity]
            imag_t = owned[capacity:]
            for source in range(2):
                real_s = source_ref[member, 2 * source : 2 * source + 1]
                imag_s = source_ref[member, 2 * source + 1 : 2 * source + 2]
                even = real_t * real_s + imag_t * imag_s
                odd = real_t * imag_s - imag_t * real_s
                even_fold = even[:, :PERIOD]
                odd_fold = odd[:, :PERIOD]
                for fold in range(1, folds):
                    even_fold = even_fold + even[:, fold * PERIOD : (fold + 1) * PERIOD]
                    odd_fold = odd_fold + odd[:, fold * PERIOD : (fold + 1) * PERIOD]
                row = member * rows + (source * offsets + offset) * capacity
                cross_ref[row : row + capacity, :PERIOD] = even_fold.astype(jnp.float32)
                cross_ref[row : row + capacity, PERIOD:] = odd_fold.astype(jnp.float32)
    product = jnp.dot(
        cross_ref[...].astype(jnp.bfloat16), table_ref[...], preferred_element_type=jnp.float32
    )
    product = (product * norm_scale).astype(out_ref.dtype)
    for member in range(group):
        out_ref[member] = product[member * rows : (member + 1) * rows]


def correlate(placed, white_sources, table, offsets, capacity):
    blocks, _, group_bins = placed.shape
    rows = 2 * offsets * capacity
    lags_out = table.shape[1]
    group = 8
    body = functools.partial(correlate_kernel, blocks, offsets, capacity, group, BINS ** (-0.5))
    return pl.pallas_call(
        body,
        grid=(blocks // group,),
        in_specs=[
            pl.BlockSpec(placed.shape, lambda a: (0, 0, 0)),
            pl.BlockSpec((group,) + white_sources.shape[1:], lambda a: (a, 0, 0)),
            pl.BlockSpec(table.shape, lambda a: (0, 0)),
        ],
        out_specs=pl.BlockSpec((group, rows, lags_out), lambda a: (a, 0, 0)),
        out_shape=jax.ShapeDtypeStruct((blocks, rows, lags_out), jnp.bfloat16),
        scratch_shapes=[pltpu.VMEM((group * rows, 2 * PERIOD), jnp.float32)],
        cost_estimate=pl.CostEstimate(
            flops=blocks * rows * 2 * PERIOD * lags_out * 2 + blocks * offsets * 16 * capacity * group_bins,
            bytes_accessed=placed.size * 2 + white_sources.size * 2 + table.size * 2 + blocks * rows * lags_out * 2,
            transcendentals=0,
        ),
    )(placed, white_sources, table)


def twiddle_table(lags_out):
    bin_index = np.arange(PERIOD, dtype=np.int64)
    lag_value = (np.arange(lags_out, dtype=np.int64) - lags_out // 2) * DEC
    phase = np.mod(bin_index[:, None] * lag_value[None, :], BINS).astype(np.float32)
    phase = (phase * np.float32(2.0 * math.pi / BINS)).astype(np.float64)
    table = np.concatenate([np.cos(phase), np.sin(phase)], axis=0)
    return table.astype(ml_dtypes.bfloat16)


def per_device(traces, sources, owner):
    blocks = lax.axis_size("blk")
    band_count = lax.axis_size("band")
    station_count = traces.shape[0]
    source_count = sources.shape[0]
    group_bins = traces.shape[2]
    capacity = max(2, 2 * station_count // blocks)
    lags_out = LAGS // DEC
    offsets = blocks // 4
    band = lax.axis_index("band")

    source_float = sources.astype(jnp.float32)
    source_sums = jnp.sum(source_float * source_float, axis=(1, 2))
    source_power = source_sums + lax.ppermute(source_sums, "band", [(0, 1), (1, 0)])
    trace_float = traces.astype(jnp.float32)
    trace_power = lax.psum(jnp.sum(trace_float * trace_float, axis=(1, 2)), "band")
    white_sources = (
        source_float * lax.rsqrt(source_power / (2 * BINS) + EPS)[:, None, None]
    ).astype(jnp.bfloat16)
    me = lax.axis_index("blk")
    held = white_sources[None]
    bits = blocks.bit_length() - 1
    shift = bits
    while shift > 0:
        width = 2 if shift >= 2 else 1
        shift -= width
        radix = 1 << width
        position = jnp.bitwise_and(me >> shift, radix - 1)
        widened = jnp.zeros((radix,) + held.shape, held.dtype)
        for partner in range(radix):
            if partner == 0:
                got = held
            else:
                route = [(i, i ^ (partner << shift)) for i in range(blocks)]
                got = lax.ppermute(held, "blk", route)
            widened = lax.dynamic_update_slice_in_dim(
                widened, got[None], jnp.bitwise_xor(position, partner), axis=0
            )
        held = widened
    groups = held.ndim - white_sources.ndim
    held = held.transpose(tuple(reversed(range(groups))) + tuple(range(groups, held.ndim)))
    owners = owner[:, 0]
    owner_hits = (owners[:, None] == jnp.arange(blocks, dtype=jnp.int32)[None, :]).astype(jnp.int32)
    earlier = jnp.cumsum(owner_hits, axis=0) - owner_hits
    arrival = jnp.sum(owner_hits * earlier, axis=1)
    slot_index = owners * capacity + arrival
    chosen = jnp.arange(blocks * capacity, dtype=jnp.int32)[:, None] == slot_index[None, :]
    raw_placed = jnp.dot(
        chosen.astype(jnp.bfloat16), traces.reshape(station_count, 2 * group_bins),
        preferred_element_type=jnp.float32,
    )
    station_scale = lax.rsqrt(trace_power / (2 * BINS) + EPS)
    slot_scale = jnp.sum(jnp.where(chosen, station_scale[None, :], 0.0), axis=1)
    placed = (raw_placed * slot_scale[:, None]).astype(jnp.bfloat16)
    placed = placed.reshape(blocks, capacity, 2, group_bins).transpose(0, 2, 1, 3)
    placed = placed.reshape(blocks, 2 * capacity, group_bins)

    table = jnp.asarray(twiddle_table(lags_out))

    white_sources = held.reshape(blocks, source_count * 2, group_bins)

    partial = correlate(placed, white_sources, table, offsets, capacity)
    arrived = lax.all_to_all(partial, "blk", split_axis=0, concat_axis=0, tiled=True)
    half = blocks // 2
    mine = lax.dynamic_slice_in_dim(arrived, band * half, half, axis=0)
    other = lax.dynamic_slice_in_dim(arrived, (1 - band) * half, half, axis=0)
    other = lax.ppermute(other, "band", [(0, 1), (1, 0)])
    summed = mine.astype(jnp.float32) + other.astype(jnp.float32)
    summed = summed.reshape(half, source_count, offsets, capacity, lags_out)
    return jnp.transpose(summed, (1, 2, 0, 3, 4)).reshape(
        source_count, offsets, half * capacity, lags_out
    )


def solution(mesh):
    placed = (P("blk", None, "band"), P("blk", None, "band"), P("blk", None))
    return jax.shard_map(
        per_device,
        mesh=mesh,
        in_specs=placed,
        out_specs=P("blk", None, "band", None),
        check_vma=False,
    )
```

```python
import functools
import math

import jax
import ml_dtypes
import numpy as np
import jax.numpy as jnp
from jax import lax
from jax.experimental import pallas as pl
from jax.experimental.pallas import tpu as pltpu
from jax.sharding import PartitionSpec as P

BINS = 8192
LAGS = 2048
DEC = 8
PERIOD = BINS // DEC


EPS = 1e-06


def correlate_kernel(blocks, offsets, capacity, group, norm_scale, placed_ref, source_ref, table_ref, out_ref, cross_ref):
    first = pl.program_id(0) * group
    folds = placed_ref.shape[2] // PERIOD
    rows = 2 * offsets * capacity
    for member in range(group):
        block = first + member
        for offset in range(offsets):
            owned = placed_ref[lax.rem(block - offset + blocks, blocks)]
            real_t = owned[:capacity]
            imag_t = owned[capacity:]
            for source in range(2):
                real_s = source_ref[member, 2 * source : 2 * source + 1]
                imag_s = source_ref[member, 2 * source + 1 : 2 * source + 2]
                even = real_t * real_s + imag_t * imag_s
                odd = real_t * imag_s - imag_t * real_s
                even_fold = even[:, :PERIOD]
                odd_fold = odd[:, :PERIOD]
                for fold in range(1, folds):
                    even_fold = even_fold + even[:, fold * PERIOD : (fold + 1) * PERIOD]
                    odd_fold = odd_fold + odd[:, fold * PERIOD : (fold + 1) * PERIOD]
                row = member * rows + (source * offsets + offset) * capacity
                cross_ref[row : row + capacity, :PERIOD] = even_fold.astype(jnp.float32)
                cross_ref[row : row + capacity, PERIOD:] = odd_fold.astype(jnp.float32)
    product = jnp.dot(
        cross_ref[...].astype(jnp.bfloat16), table_ref[...], preferred_element_type=jnp.float32
    )
    product = product.astype(out_ref.dtype)
    for member in range(group):
        out_ref[member] = product[member * rows : (member + 1) * rows]


def correlate(placed, white_sources, table, offsets, capacity):
    blocks, _, group_bins = placed.shape
    rows = 2 * offsets * capacity
    lags_out = table.shape[1]
    group = 8
    body = functools.partial(correlate_kernel, blocks, offsets, capacity, group, BINS ** (-0.5))
    return pl.pallas_call(
        body,
        grid=(blocks // group,),
        in_specs=[
            pl.BlockSpec(placed.shape, lambda a: (0, 0, 0)),
            pl.BlockSpec((group,) + white_sources.shape[1:], lambda a: (a, 0, 0)),
            pl.BlockSpec(table.shape, lambda a: (0, 0)),
        ],
        out_specs=pl.BlockSpec((group, rows, lags_out), lambda a: (a, 0, 0)),
        out_shape=jax.ShapeDtypeStruct((blocks, rows, lags_out), jnp.bfloat16),
        scratch_shapes=[pltpu.VMEM((group * rows, 2 * PERIOD), jnp.float32)],
        cost_estimate=pl.CostEstimate(
            flops=blocks * rows * 2 * PERIOD * lags_out * 2 + blocks * offsets * 16 * capacity * group_bins,
            bytes_accessed=placed.size * 2 + white_sources.size * 2 + table.size * 2 + blocks * rows * lags_out * 2,
            transcendentals=0,
        ),
    )(placed, white_sources, table)


def twiddle_table(lags_out):
    bin_index = np.arange(PERIOD, dtype=np.int64)
    lag_value = (np.arange(lags_out, dtype=np.int64) - lags_out // 2) * DEC
    phase = np.mod(bin_index[:, None] * lag_value[None, :], BINS).astype(np.float32)
    phase = (phase * np.float32(2.0 * math.pi / BINS)).astype(np.float64)
    table = np.concatenate([np.cos(phase), np.sin(phase)], axis=0) * BINS ** (-0.5)
    return table.astype(ml_dtypes.bfloat16)


def per_device(traces, sources, owner):
    blocks = lax.axis_size("blk")
    band_count = lax.axis_size("band")
    station_count = traces.shape[0]
    source_count = sources.shape[0]
    group_bins = traces.shape[2]
    capacity = max(2, 2 * station_count // blocks)
    lags_out = LAGS // DEC
    offsets = blocks // 4
    band = lax.axis_index("band")

    trace_float = traces.astype(jnp.float32)
    source_float = sources.astype(jnp.float32)
    trace_power, source_power = lax.psum(
        (
            jnp.sum(trace_float * trace_float, axis=(1, 2)),
            jnp.sum(source_float * source_float, axis=(1, 2)),
        ),
        "band",
    )
    white_sources = (
        source_float * lax.rsqrt(source_power / (2 * BINS) + EPS)[:, None, None]
    ).astype(jnp.bfloat16)
    me = lax.axis_index("blk")
    held = white_sources[None]
    bits = blocks.bit_length() - 1
    shift = bits
    while shift > 0:
        width = 2 if shift >= 2 else 1
        shift -= width
        radix = 1 << width
        position = jnp.bitwise_and(me >> shift, radix - 1)
        widened = jnp.zeros((radix,) + held.shape, held.dtype)
        for partner in range(radix):
            if partner == 0:
                got = held
            else:
                route = [(i, i ^ (partner << shift)) for i in range(blocks)]
                got = lax.ppermute(held, "blk", route)
            widened = lax.dynamic_update_slice_in_dim(
                widened, got[None], jnp.bitwise_xor(position, partner), axis=0
            )
        held = widened
    groups = held.ndim - white_sources.ndim
    held = held.transpose(tuple(reversed(range(groups))) + tuple(range(groups, held.ndim)))
    owners = owner[:, 0]
    owner_hits = (owners[:, None] == jnp.arange(blocks, dtype=jnp.int32)[None, :]).astype(jnp.int32)
    earlier = jnp.cumsum(owner_hits, axis=0) - owner_hits
    arrival = jnp.sum(owner_hits * earlier, axis=1)
    slot_index = owners * capacity + arrival
    chosen = jnp.arange(blocks * capacity, dtype=jnp.int32)[:, None] == slot_index[None, :]
    raw_placed = jnp.dot(
        chosen.astype(jnp.bfloat16), traces.reshape(station_count, 2 * group_bins),
        preferred_element_type=jnp.float32,
    )
    station_scale = lax.rsqrt(trace_power / (2 * BINS) + EPS)
    slot_scale = jnp.sum(jnp.where(chosen, station_scale[None, :], 0.0), axis=1)
    placed = (raw_placed * slot_scale[:, None]).astype(jnp.bfloat16)
    placed = placed.reshape(blocks, capacity, 2, group_bins).transpose(0, 2, 1, 3)
    placed = placed.reshape(blocks, 2 * capacity, group_bins)

    table = jnp.asarray(twiddle_table(lags_out))

    white_sources = held.reshape(blocks, source_count * 2, group_bins)

    partial = correlate(placed, white_sources, table, offsets, capacity)
    arrived = lax.all_to_all(partial, "blk", split_axis=0, concat_axis=0, tiled=True)
    half = blocks // 2
    mine = lax.dynamic_slice_in_dim(arrived, band * half, half, axis=0)
    other = lax.dynamic_slice_in_dim(arrived, (1 - band) * half, half, axis=0)
    other = lax.ppermute(other, "band", [(0, 1), (1, 0)])
    summed = mine.astype(jnp.float32) + other.astype(jnp.float32)
    summed = summed.reshape(half, source_count, offsets, capacity, lags_out)
    return jnp.transpose(summed, (1, 2, 0, 3, 4)).reshape(
        source_count, offsets, half * capacity, lags_out
    )


def solution(mesh):
    placed = (P("blk", None, "band"), P("blk", None, "band"), P("blk", None))
    return jax.shard_map(
        per_device,
        mesh=mesh,
        in_specs=placed,
        out_specs=P("blk", None, "band", None),
        check_vma=False,
    )
```

```python
import functools
import math

import jax
import ml_dtypes
import numpy as np
import jax.numpy as jnp
from jax import lax
from jax.experimental import pallas as pl
from jax.experimental.pallas import tpu as pltpu
from jax.sharding import PartitionSpec as P

BINS = 8192
LAGS = 2048
DEC = 8
PERIOD = BINS // DEC


EPS = 1e-06


def correlate_kernel(blocks, offsets, capacity, group, norm_scale, placed_ref, source_ref, table_ref, out_ref, cross_ref):
    first = pl.program_id(0) * group
    folds = placed_ref.shape[2] // PERIOD
    rows = 2 * offsets * capacity
    for member in range(group):
        block = first + member
        for offset in range(offsets):
            owned = placed_ref[lax.rem(block - offset + blocks, blocks)]
            real_t = owned[:capacity]
            imag_t = owned[capacity:]
            for source in range(2):
                real_s = source_ref[member, 2 * source : 2 * source + 1]
                imag_s = source_ref[member, 2 * source + 1 : 2 * source + 2]
                even = real_t * real_s + imag_t * imag_s
                odd = real_t * imag_s - imag_t * real_s
                even_fold = even[:, :PERIOD]
                odd_fold = odd[:, :PERIOD]
                for fold in range(1, folds):
                    even_fold = even_fold + even[:, fold * PERIOD : (fold + 1) * PERIOD]
                    odd_fold = odd_fold + odd[:, fold * PERIOD : (fold + 1) * PERIOD]
                row = member * rows + (source * offsets + offset) * capacity
                cross_ref[row : row + capacity, :PERIOD] = even_fold
                cross_ref[row : row + capacity, PERIOD:] = odd_fold
    product = jnp.dot(
        cross_ref[...], table_ref[...], preferred_element_type=jnp.float32
    )
    product = (product * norm_scale).astype(out_ref.dtype)
    for member in range(group):
        out_ref[member] = product[member * rows : (member + 1) * rows]


def correlate(placed, white_sources, table, offsets, capacity):
    blocks, _, group_bins = placed.shape
    rows = 2 * offsets * capacity
    lags_out = table.shape[1]
    group = 8
    body = functools.partial(correlate_kernel, blocks, offsets, capacity, group, BINS ** (-0.5))
    return pl.pallas_call(
        body,
        grid=(blocks // group,),
        in_specs=[
            pl.BlockSpec(placed.shape, lambda a: (0, 0, 0)),
            pl.BlockSpec((group,) + white_sources.shape[1:], lambda a: (a, 0, 0)),
            pl.BlockSpec(table.shape, lambda a: (0, 0)),
        ],
        out_specs=pl.BlockSpec((group, rows, lags_out), lambda a: (a, 0, 0)),
        out_shape=jax.ShapeDtypeStruct((blocks, rows, lags_out), jnp.bfloat16),
        scratch_shapes=[pltpu.VMEM((group * rows, 2 * PERIOD), jnp.bfloat16)],
        cost_estimate=pl.CostEstimate(
            flops=blocks * rows * 2 * PERIOD * lags_out * 2 + blocks * offsets * 16 * capacity * group_bins,
            bytes_accessed=placed.size * 2 + white_sources.size * 2 + table.size * 2 + blocks * rows * lags_out * 2,
            transcendentals=0,
        ),
    )(placed, white_sources, table)


def twiddle_table(lags_out):
    bin_index = np.arange(PERIOD, dtype=np.int64)
    lag_value = (np.arange(lags_out, dtype=np.int64) - lags_out // 2) * DEC
    phase = np.mod(bin_index[:, None] * lag_value[None, :], BINS).astype(np.float32)
    phase = (phase * np.float32(2.0 * math.pi / BINS)).astype(np.float64)
    table = np.concatenate([np.cos(phase), np.sin(phase)], axis=0)
    return table.astype(ml_dtypes.bfloat16)


def per_device(traces, sources, owner):
    blocks = lax.axis_size("blk")
    band_count = lax.axis_size("band")
    station_count = traces.shape[0]
    source_count = sources.shape[0]
    group_bins = traces.shape[2]
    capacity = max(2, 2 * station_count // blocks)
    lags_out = LAGS // DEC
    offsets = blocks // 4
    band = lax.axis_index("band")

    trace_float = traces.astype(jnp.float32)
    source_float = sources.astype(jnp.float32)
    trace_power, source_power = lax.psum(
        (
            jnp.sum(trace_float * trace_float, axis=(1, 2)),
            jnp.sum(source_float * source_float, axis=(1, 2)),
        ),
        "band",
    )
    white_sources = (
        source_float * lax.rsqrt(source_power / (2 * BINS) + EPS)[:, None, None]
    ).astype(jnp.bfloat16)
    me = lax.axis_index("blk")
    held = white_sources[None]
    bits = blocks.bit_length() - 1
    shift = bits
    while shift > 0:
        width = 2 if shift >= 2 else 1
        shift -= width
        radix = 1 << width
        position = jnp.bitwise_and(me >> shift, radix - 1)
        widened = jnp.zeros((radix,) + held.shape, held.dtype)
        for partner in range(radix):
            if partner == 0:
                got = held
            else:
                route = [(i, i ^ (partner << shift)) for i in range(blocks)]
                got = lax.ppermute(held, "blk", route)
            widened = lax.dynamic_update_slice_in_dim(
                widened, got[None], jnp.bitwise_xor(position, partner), axis=0
            )
        held = widened
    groups = held.ndim - white_sources.ndim
    held = held.transpose(tuple(reversed(range(groups))) + tuple(range(groups, held.ndim)))
    owners = owner[:, 0]
    owner_hits = (owners[:, None] == jnp.arange(blocks, dtype=jnp.int32)[None, :]).astype(jnp.int32)
    earlier = jnp.cumsum(owner_hits, axis=0) - owner_hits
    arrival = jnp.sum(owner_hits * earlier, axis=1)
    slot_index = owners * capacity + arrival
    chosen = jnp.arange(blocks * capacity, dtype=jnp.int32)[:, None] == slot_index[None, :]
    raw_placed = jnp.dot(
        chosen.astype(jnp.bfloat16), traces.reshape(station_count, 2 * group_bins),
        preferred_element_type=jnp.float32,
    )
    station_scale = lax.rsqrt(trace_power / (2 * BINS) + EPS)
    slot_scale = jnp.sum(jnp.where(chosen, station_scale[None, :], 0.0), axis=1)
    placed = (raw_placed * slot_scale[:, None]).astype(jnp.bfloat16)
    placed = placed.reshape(blocks, capacity, 2, group_bins).transpose(0, 2, 1, 3)
    placed = placed.reshape(blocks, 2 * capacity, group_bins)

    table = jnp.asarray(twiddle_table(lags_out))

    white_sources = held.reshape(blocks, source_count * 2, group_bins)

    partial = correlate(placed, white_sources, table, offsets, capacity)
    arrived = lax.all_to_all(partial, "blk", split_axis=0, concat_axis=0, tiled=True)
    half = blocks // 2
    mine = lax.dynamic_slice_in_dim(arrived, band * half, half, axis=0)
    other = lax.dynamic_slice_in_dim(arrived, (1 - band) * half, half, axis=0)
    other = lax.ppermute(other, "band", [(0, 1), (1, 0)])
    summed = mine.astype(jnp.float32) + other.astype(jnp.float32)
    summed = summed.reshape(half, source_count, offsets, capacity, lags_out)
    return jnp.transpose(summed, (1, 2, 0, 3, 4)).reshape(
        source_count, offsets, half * capacity, lags_out
    )


def solution(mesh):
    placed = (P("blk", None, "band"), P("blk", None, "band"), P("blk", None))
    return jax.shard_map(
        per_device,
        mesh=mesh,
        in_specs=placed,
        out_specs=P("blk", None, "band", None),
        check_vma=False,
    )
```
